512 devices in a mesh: dp: 128 (over y, z, core), tp: 4 (over x).
Axes of the slice: x: 4, y: 8, z: 8, core: 2. Of those that a mesh axis runs over, the one named last changes fastest.
Arguments:
- hidden: bfloat16 [2048, 2048], P('dp'), may hold values from -6 to 6
- routes: int32 [2048, 8], P('dp'), may hold values from 0 to 127, all different within a row; in each aligned block of 16 rows (0 to 15, 16 to 31, ...) at most 2 rows name the same one
- route_weights: int32 [2048, 8], P('dp'), may hold values from 1 to 65535
- w_gate: bfloat16 [128, 2048, 1024], P('dp', None, 'tp'), may hold values from -0.125 to 0.125
- w_up: bfloat16 [128, 2048, 1024], P('dp', None, 'tp'), may hold values from -0.125 to 0.125
- w_down: bfloat16 [128, 1024, 2048], P('dp', 'tp'), may hold values from -0.1875 to 0.1875
- queries: bfloat16 [1024, 8192], P('dp', 'tp'), may hold values from -480 to 480
- key_codes: bfloat16 [262144, 512], P('dp', 'tp'), may hold values from -127 to 127, as said below
- key_scales: float32 [4, 262144], P('tp', 'dp'), may hold values from 0.004 to 0.02
- cache_values: bfloat16 [262144, 512], P('dp', 'tp'), may hold values from -6 to 6
- new_keys: bfloat16 [1024, 512], P('dp', 'tp'), may hold values from -6 to 6
- new_values: bfloat16 [1024, 512], P('dp', 'tp'), may hold values from -6 to 6
- lengths: int32 [1024], P('dp'), may hold values from 1 to 2041, as said below
Outputs:
- expert_mix: bfloat16 [2048, 2048], P('dp')
- attended: bfloat16 [1024, 8192], P('dp', 'tp')
The draws below stay inside these ranges and needn't reach their ends.
Inputs may be any that keep to these rules, and one draw needn't show every extreme that they name: `lengths`: the 8 requests of each block sum to at most 2048 positions; in every draw some block sums to exactly 2048, one of its requests holding 2048 - 7 positions. `routes`: each row names 8 different experts. Among the rows of one index of dp no expert is named more than 2 times, and in every draw some expert is named exactly 2 times by the rows of some index. `key_codes`: whole numbers.
All inputs are finite; a program needn't handle non-finite values.
Results may differ from the reference program's by a relative error of at most 0.014.
The reference program's roundings to bfloat16 on the way count: a program that leaves them out, or rounds other values in their place, can miss the bound.
Values may be sent and summed in bfloat16 or wider, within the bound.
No kernel may reach another device: no remote copies, remote signals or barrier semaphores. Data moves between devices by JAX's collectives and lax.ppermute only.
A program may use at most 64 MiB of HBM per device.

```python
import math
import jax
import jax.numpy as jnp
import numpy as np
from jax import lax

D = 2048
QH = 64
KVH = 4
HEAD = 128
FFE = 1024
TOPK = 8
TOK_DEV = 16
REQ_DEV = 8
CAP = 2048
EXPERTS = 128
TOKENS = 2048
REQS = 1024
CACHE = 262144
MOST = 2
N_DP = 128
N_TP = 4


def draw_lengths(key, part):
    devices = REQS // REQ_DEV
    key_total, key_full, key_share = jax.random.split(key, 3)
    totals = jax.random.randint(key_total, (devices,), CAP // 8, CAP + 1)
    chosen = jax.random.randint(key_full, (), 0, devices)
    totals = jnp.where(jnp.arange(devices) == chosen, CAP, totals)
    shares = jax.random.randint(key_share, (devices, REQ_DEV), 1, 33)
    surplus = totals - REQ_DEV
    pieces = 1 + surplus[:, None] * shares // jnp.sum(shares, axis=1, keepdims=True)
    missing = totals - jnp.sum(pieces, axis=1)
    closing = jnp.arange(REQ_DEV) == REQ_DEV - 1
    pieces = pieces + jnp.where(closing[None, :], missing[:, None], 0)
    long_row = jnp.where(closing, CAP - REQ_DEV + 1, 1)
    is_chosen = (jnp.arange(devices) == chosen)[:, None]
    pieces = jnp.where(is_chosen, long_row[None, :], pieces)
    return pieces.reshape(-1).astype(jnp.int32)


def draw_key_codes(key, part):
    codes = jax.random.randint(key, (CACHE, KVH * HEAD), -127, 128)
    return codes.astype(jnp.float32).astype(jnp.bfloat16)


def draw_queries(key, part):
    key_base = jax.random.fold_in(key, 0)
    drawn = jnp.clip(jax.random.normal(key_base, (REQS, QH * HEAD), jnp.float32), -6.0, 6.0)
    return drawn.astype(jnp.bfloat16)


def with_ends(entries, rng, low, largest):
    longest = entries.shape.index(max(entries.shape))
    spots = []
    for shift in (0, 1):
        where = [jax.random.randint(jax.random.fold_in(rng, axis), (), 0, length) for axis, length in enumerate(entries.shape)]
        where[longest] = (where[longest] + shift) % entries.shape[longest]
        spots.append(tuple(where))
    return entries.at[spots[0]].set(low).at[spots[1]].set(largest)


def shard_levels(own_key, extent, cuts, smallest, top_value):
    gain, own = 1.0, jax.random.fold_in(own_key, 6)
    for dim, blocks in cuts:
        steps = jnp.exp(jax.random.uniform(jax.random.fold_in(own, dim), (blocks,), jnp.float32, smallest / len(cuts), top_value / len(cuts)))
        gain = gain * jnp.repeat(steps, extent[dim] // blocks).reshape([-1 if axis == dim else 1 for axis in range(len(extent))])
    return gain


def assign_block(key, own, number, rows, amount, top, most, slope):
    order = jax.random.permutation(key, amount)
    packed, common = portions_of(amount, rows * top, most, slope, True), portions_of(amount, rows * top, most, slope, False)
    places = jnp.arange(amount)

    def named(tallies, rotation):
        used = int((tallies > 0).sum())
        fixed = max(1, used // 4)
        shifted = fixed + (places - fixed + rotation * (used - fixed)) % max(1, amount - fixed)
        return jnp.zeros((amount,), jnp.int32).at[order[jnp.where(places < fixed, places, shifted)]].set(jnp.asarray(tallies, jnp.int32))

    tallies = jnp.where(number % 4 == 0, named(packed, number // 4), named(common, number - number // 4 - 1))
    mixed = jax.random.permutation(jax.random.fold_in(own, 3), amount)
    giver, sink = mixed[0:amount // 2 * 2:2], mixed[1:amount // 2 * 2:2]
    slack = jnp.minimum(tallies[giver] - 1, most - tallies[sink]) // 2
    slack = jnp.where((giver == order[0]) | (sink == order[0]) | (tallies[sink] == 0), 0, jnp.maximum(slack, 0))
    shifted = jax.random.randint(jax.random.fold_in(own, 4), (amount // 2,), 0, 1 << 20) % (slack + 1)
    tallies = tallies.at[giver].add(-shifted).at[sink].add(shifted)
    members = jnp.searchsorted(jnp.cumsum(tallies), jnp.arange(rows * top), side="right").astype(jnp.int32)
    grid = members.reshape(top, rows).T
    grid = grid[jax.random.permutation(jax.random.fold_in(own, 1), rows)]
    rotation = jax.random.randint(jax.random.fold_in(own, 2), (rows, 1), 0, top)
    return jnp.take_along_axis(grid, (jnp.arange(top)[None, :] + rotation) % top, axis=1)


def portions_of(count, total, bound, slope, full):
    weights = [(1 << 20) // math.isqrt(rank ** slope) + 1 for rank in range(1, count + 1)]
    largest = bound if full else min(bound, max(-(-total // count), total * weights[0] // sum(weights)))
    least = 1 if total - largest >= count - 1 else 0
    counts, spare = [largest] + [least] * (count - 1), total - largest - least * (count - 1)
    while spare > 0:
        free = [i for i in range(1, count) if counts[i] < largest] or [i for i in range(1, count) if counts[i] < bound]
        mass, left = sum([weights[i] for i in free]), spare
        for i in free:
            more = min(bound - counts[i], max(1, left * weights[i] // mass), spare)
            counts[i] = counts[i] + more
            spare = spare - more
    return np.array(counts)


def bell_draw(own_key, shape, deviation, reach, shards=(), kind=jnp.bfloat16):
    values = jax.random.normal(own_key, shape, jnp.float32) * deviation
    if len(shards) > 0:
        values = shard_levels(own_key, shape, shards, -0.22, 0.18) * values
    return jnp.clip(values, min=-reach, max=reach).astype(kind)


def setup_inputs(seed: int = 0) -> dict:
    streams_of = jax.random.split(jax.random.key(seed), 14)
    hidden = bell_draw(streams_of[0], (TOKENS, D), 1.0, 6.0, ((0, 128),))
    routes_keys = jax.random.split(jax.random.fold_in(streams_of[1], 1), TOKENS // TOK_DEV)
    routes_turns = jax.random.permutation(jax.random.fold_in(streams_of[1], 3), TOKENS // TOK_DEV)
    routes = jax.vmap(lambda own, number: assign_block(jax.random.fold_in(streams_of[1], 2), own, number, TOK_DEV, EXPERTS, TOPK, MOST, 2))(routes_keys, routes_turns).reshape((TOKENS, TOPK))
    route_weights = with_ends(jax.random.randint(streams_of[2], (TOKENS, TOPK), 1, 65536), jax.random.fold_in(streams_of[2], 1), 1, 65535).astype(jnp.int32)
    w_gate = bell_draw(streams_of[3], (EXPERTS, D, FFE), D ** -0.5, 0.125, ((0, 128), (2, 4)))
    w_up = bell_draw(streams_of[4], (EXPERTS, D, FFE), D ** -0.5, 0.125, ((0, 128), (2, 4)))
    w_down = bell_draw(streams_of[5], (EXPERTS, FFE, D), FFE ** -0.5, 0.1875, ((0, 128), (1, 4)))
    queries = draw_queries(jax.random.fold_in(streams_of[13], 71), 0)
    key_codes = draw_key_codes(jax.random.fold_in(streams_of[13], 71), 0)
    key_scales = jnp.clip(jnp.exp(math.log(0.02) - 1.6094378 * jax.random.uniform(streams_of[8], (KVH, CACHE), jnp.float32) ** shard_levels(streams_of[8], (KVH, CACHE), ((0, 4), (1, 128)), -0.2, 0.2)), 0.004, 0.02)
    cache_values = bell_draw(streams_of[9], (CACHE, KVH * HEAD), 1.0, 6.0, ((0, 128), (1, 4)))
    new_keys = bell_draw(streams_of[10], (REQS, KVH * HEAD), 1.0, 6.0, ((0, 128), (1, 4)))
    new_values = bell_draw(streams_of[11], (REQS, KVH * HEAD), 1.0, 6.0, ((0, 128), (1, 4)))
    lengths = draw_lengths(jax.random.fold_in(streams_of[13], 71), 0)
    return {"hidden": hidden, "routes": routes, "route_weights": route_weights, "w_gate": w_gate, "w_up": w_up, "w_down": w_down, "queries": queries, "key_codes": key_codes, "key_scales": key_scales, "cache_values": cache_values, "new_keys": new_keys, "new_values": new_values, "lengths": lengths}


rope_base = 1000000.0


def rounded(value):
    return lax.optimization_barrier(value.astype(jnp.bfloat16)).astype(jnp.float32)


def inverse_freq(head_size):
    steps = jnp.arange(head_size // 2, dtype=jnp.float32) * (2.0 / head_size)
    return jnp.exp(-steps * jnp.log(jnp.float32(rope_base)))


def rotate(vector, angles):
    half_size = vector.shape[-1] // 2
    front_half = vector[..., :half_size]
    back_half = vector[..., half_size:]
    cosine = jnp.cos(angles)
    sine_part = jnp.sin(angles)
    return jnp.concatenate([front_half * cosine - back_half * sine_part, back_half * cosine + front_half * sine_part], axis=-1)


def attend_device(queries, codes, scales, cache_values, new_keys, new_values, lengths):
    row_count = queries.shape[0]
    cache_len = codes.shape[0]
    groups = scales.shape[0]
    head_size = codes.shape[1] // groups
    per_group = queries.shape[1] // (groups * head_size)
    lengths = lengths.astype(jnp.int32)
    request_end = jnp.cumsum(lengths).astype(jnp.int32)
    starts = (request_end - lengths).astype(jnp.int32)
    cache_pos = jnp.arange(cache_len, dtype=jnp.int32)
    member = (cache_pos[:, None] >= starts[None, :]) & (cache_pos[:, None] < request_end[None, :])
    offset = jnp.sum(jnp.where(member, starts[None, :], 0), axis=1).astype(jnp.int32)
    position = (cache_pos - offset).astype(jnp.float32)
    frequency = inverse_freq(head_size)
    key_angles = position[:, None, None] * frequency[None, None, :]
    cache_keys = codes.astype(jnp.float32).reshape(cache_len, groups, head_size) * jnp.transpose(scales)[:, :, None]
    cache_keys = rounded(rotate(cache_keys, key_angles))
    query_angles = lengths.astype(jnp.float32)[:, None] * frequency[None, :]
    rotated_query = queries.astype(jnp.float32).reshape(row_count, groups, per_group, head_size)
    rotated_query = rounded(rotate(rotated_query, query_angles[:, None, None, :]))
    fresh_key = rounded(rotate(new_keys.astype(jnp.float32).reshape(row_count, groups, head_size), query_angles[:, None, :]))
    score_scale = head_size ** -0.5
    scores = jnp.einsum("rgqd,cgd->rgqc", rotated_query, cache_keys) * score_scale
    own_score = jnp.einsum("rgqd,rgd->rgq", rotated_query, fresh_key) * score_scale
    live_mask = jnp.transpose(member)[:, None, None, :]
    scores = jnp.where(live_mask, scores, -jnp.inf)
    peak_score = jnp.maximum(jnp.max(scores, axis=-1), own_score)
    weights = jnp.exp(scores - peak_score[..., None])
    own_weight = jnp.exp(own_score - peak_score)
    weight_sum = jnp.sum(weights, axis=-1) + own_weight
    value_rows = cache_values.astype(jnp.float32).reshape(cache_len, groups, head_size)
    mixture = jnp.einsum("rgqc,cgd->rgqd", rounded(weights), value_rows)
    mixture = mixture + own_weight[..., None] * new_values.astype(jnp.float32).reshape(row_count, groups, 1, head_size)
    return (mixture / weight_sum[..., None]).reshape(row_count, groups * per_group * head_size).astype(jnp.bfloat16)


def attend_bundle(bundle):
    return attend_device(bundle[0], bundle[1], bundle[2], bundle[3], bundle[4], bundle[5], bundle[6])


def attend_all(queries, key_codes, key_scales, cache_values, new_keys, new_values, lengths):
    devices = lengths.shape[0] // REQ_DEV
    stacked = (queries.reshape(devices, REQ_DEV, -1),
               key_codes.reshape(devices, CAP, -1),
               jnp.transpose(key_scales.reshape(KVH, devices, CAP), (1, 0, 2)),
               cache_values.reshape(devices, CAP, -1),
               new_keys.reshape(devices, REQ_DEV, -1),
               new_values.reshape(devices, REQ_DEV, -1),
               lengths.reshape(devices, REQ_DEV))
    result = lax.map(attend_bundle, stacked)
    return result.reshape(devices * REQ_DEV, -1)


def expert_mixture(hidden, routes, route_weights, w_gate, w_up, w_down):
    flat_ids = routes.reshape(N_DP, TOK_DEV * TOPK).astype(jnp.int32)
    onehot = (flat_ids[:, :, None] == jnp.arange(EXPERTS, dtype=jnp.int32)[None, None, :]).astype(jnp.int32)
    rank_ids = jnp.sum(onehot * (jnp.cumsum(onehot, axis=1) - 1), axis=2).astype(jnp.int32)
    source = jnp.arange(N_DP, dtype=jnp.int32)[:, None]
    slot_ids = (source * MOST + rank_ids).astype(jnp.int32)
    token_id = (source * TOK_DEV + jnp.arange(TOK_DEV * TOPK, dtype=jnp.int32)[None, :] // TOPK).astype(jnp.int32)
    slot_table = jnp.full((EXPERTS, N_DP * MOST), TOKENS, jnp.int32).at[flat_ids, slot_ids].set(token_id)
    padded = jnp.concatenate([hidden, jnp.zeros((1, D), jnp.bfloat16)], axis=0)

    def one_expert(bundle):
        slot_rows, gate_w, up_w, down_w = bundle
        inputs = padded[slot_rows]
        gate_act = jnp.dot(inputs, gate_w, preferred_element_type=jnp.float32)
        up_act = jnp.dot(inputs, up_w, preferred_element_type=jnp.float32)
        hidden_act = (jax.nn.silu(gate_act) * up_act).astype(jnp.bfloat16)
        block_size = FFE // N_TP
        summed = jnp.zeros((slot_rows.shape[0], D), jnp.float32)
        for block_index in range(N_TP):
            low_edge = block_index * block_size
            piece_out = jnp.dot(hidden_act[:, low_edge:low_edge + block_size], down_w[low_edge:low_edge + block_size], preferred_element_type=jnp.float32)
            summed = summed + rounded(piece_out)
        return summed.astype(jnp.bfloat16)

    results = lax.map(one_expert, (slot_table, w_gate, w_up, w_down))
    picked = results[flat_ids, slot_ids].reshape(TOKENS, TOPK, D).astype(jnp.float32)
    shares = route_weights.astype(jnp.float32)
    shares = shares / jnp.sum(shares, axis=1, keepdims=True)
    return jnp.sum(picked * shares[:, :, None], axis=1).astype(jnp.bfloat16)


def reference(hidden, routes, route_weights, w_gate, w_up, w_down, queries, key_codes, key_scales, cache_values, new_keys, new_values, lengths):
    expert_mix = expert_mixture(hidden, routes, route_weights, w_gate, w_up, w_down)
    attended = attend_all(queries, key_codes, key_scales, cache_values, new_keys, new_values, lengths)
    return (expert_mix, attended)
```

```python
import jax
import jax.numpy as jnp
from jax import lax
from jax.sharding import PartitionSpec as P

rope_base = 1000000.0


def inverse_freq(head_size):
    steps = jnp.arange(head_size // 2, dtype=jnp.float32) * (2.0 / head_size)
    return jnp.exp(-steps * jnp.log(jnp.float32(rope_base)))


def rotate(vector, angles):
    half_size = vector.shape[-1] // 2
    front_half = vector[..., :half_size]
    back_half = vector[..., half_size:]
    cosine = jnp.cos(angles)
    sine_part = jnp.sin(angles)
    return jnp.concatenate(
        [front_half * cosine - back_half * sine_part, back_half * cosine + front_half * sine_part],
        axis=-1,
    )


def attend_local(queries, codes, scales, cache_values, new_keys, new_values, lengths):
    row_count = queries.shape[0]
    cache_len = codes.shape[0]
    groups = scales.shape[0]
    head_size = codes.shape[1] // groups
    per_group = queries.shape[1] // (groups * head_size)
    request_end = jnp.cumsum(lengths)
    starts = request_end - lengths
    cache_pos = jnp.arange(cache_len, dtype=jnp.int32)
    member = (cache_pos[:, None] >= starts[None, :]) & (cache_pos[:, None] < request_end[None, :])
    offset = jnp.sum(jnp.where(member, starts[None, :], 0), axis=1)
    position = (cache_pos - offset).astype(jnp.float32)
    frequency = inverse_freq(head_size)
    cache_keys = (
        codes.astype(jnp.float32).reshape(cache_len, groups, head_size)
        * jnp.transpose(scales)[:, :, None]
    )
    cache_keys = rotate(cache_keys, position[:, None, None] * frequency[None, None, :]).astype(
        jnp.bfloat16
    )
    query_angles = lengths.astype(jnp.float32)[:, None] * frequency[None, :]
    rotated_query = queries.astype(jnp.float32).reshape(row_count, groups, per_group, head_size)
    rotated_query = rotate(rotated_query, query_angles[:, None, None, :]).astype(jnp.bfloat16)
    fresh_key = rotate(
        new_keys.astype(jnp.float32).reshape(row_count, groups, head_size), query_angles[:, None, :]
    ).astype(jnp.bfloat16)
    score_scale = head_size ** (-0.5)
    scores = (
        jnp.einsum("rgqd,cgd->rgqc", rotated_query, cache_keys, preferred_element_type=jnp.float32)
        * score_scale
    )
    own_score = (
        jnp.einsum("rgqd,rgd->rgq", rotated_query, fresh_key, preferred_element_type=jnp.float32)
        * score_scale
    )
    live_mask = jnp.transpose(member)[:, None, None, :]
    scores = jnp.where(live_mask, scores, -jnp.inf)
    peak_score = jnp.maximum(jnp.max(scores, axis=-1), own_score)
    weights = jnp.exp(scores - peak_score[..., None])
    own_weight = jnp.exp(own_score - peak_score)
    weight_sum = jnp.sum(weights, axis=-1) + own_weight
    value_rows = cache_values.reshape(cache_len, groups, head_size)
    mixture = jnp.einsum(
        "rgqc,cgd->rgqd",
        weights.astype(jnp.bfloat16),
        value_rows,
        preferred_element_type=jnp.float32,
    )
    mixture = mixture + own_weight[..., None] * new_values.astype(jnp.float32).reshape(
        row_count, groups, 1, head_size
    )
    return (
        (mixture / weight_sum[..., None])
        .reshape(row_count, groups * per_group * head_size)
        .astype(jnp.bfloat16)
    )


def expert_block(arrived, w_gate, w_up, w_down):
    arrived_shape = arrived.shape
    inputs = arrived.reshape(-1, arrived_shape[-1])
    gate_act = jnp.dot(inputs, w_gate[0], preferred_element_type=jnp.float32)
    up_act = jnp.dot(inputs, w_up[0], preferred_element_type=jnp.float32)
    hidden_act = (jax.nn.silu(gate_act) * up_act).astype(jnp.bfloat16)
    partial_value = jnp.dot(hidden_act, w_down[0], preferred_element_type=jnp.float32)
    return partial_value.reshape(arrived_shape[0], arrived_shape[1], partial_value.shape[-1])


def on_device(
    hidden,
    routes,
    route_weights,
    w_gate,
    w_up,
    w_down,
    queries,
    key_codes,
    key_scales,
    cache_values,
    new_keys,
    new_values,
    lengths,
):
    token_count = routes.shape[0]
    top_count = routes.shape[1]
    model_width = hidden.shape[1]
    tp_size = lax.axis_size("tp")
    dp_size = lax.axis_size("dp")
    slice_width = model_width // tp_size
    experts = dp_size * w_gate.shape[0]
    capacity = min(token_count, max(2, token_count * top_count * 2 // experts))
    flat_ids = routes.reshape(-1)
    onehot = (flat_ids[:, None] == jnp.arange(experts, dtype=jnp.int32)[None, :]).astype(jnp.int32)
    rank_ids = jnp.sum(onehot * (jnp.cumsum(onehot, axis=0) - 1), axis=1)
    slot_ids = flat_ids * capacity + rank_ids
    slot_grid = slot_ids.reshape(token_count, top_count)
    selector = jnp.any(
        jnp.arange(experts * capacity, dtype=jnp.int32)[:, None, None] == slot_grid[None, :, :],
        axis=2,
    ).astype(jnp.bfloat16)
    tp_index = lax.axis_index("tp")
    own_cols = lax.dynamic_slice_in_dim(hidden, tp_index * slice_width, slice_width, axis=1)
    outgoing = jnp.dot(selector, own_cols, preferred_element_type=jnp.float32).astype(jnp.bfloat16)
    outgoing = outgoing.reshape(experts, capacity, slice_width)
    arrived = lax.all_to_all(outgoing, "dp", split_axis=0, concat_axis=0, tiled=True)
    arrived = lax.all_gather(arrived, "tp", axis=0, tiled=False)
    slots = dp_size * capacity
    arrived = arrived.reshape(tp_size, slots, slice_width)
    gate_w = w_gate[0].reshape(tp_size, slice_width, w_gate.shape[2])
    up_w = w_up[0].reshape(tp_size, slice_width, w_up.shape[2])
    gate_act = jnp.einsum("tsd,tdh->sh", arrived, gate_w, preferred_element_type=jnp.float32)
    up_act = jnp.einsum("tsd,tdh->sh", arrived, up_w, preferred_element_type=jnp.float32)
    hidden_act = (jax.nn.silu(gate_act) * up_act).astype(jnp.bfloat16)
    partial_value = jnp.dot(hidden_act, w_down[0], preferred_element_type=jnp.float32)
    partial_value = partial_value.astype(jnp.bfloat16).reshape(slots, tp_size, slice_width)
    gathered = lax.all_to_all(partial_value, "tp", split_axis=1, concat_axis=1, tiled=True)
    expert_out = jnp.sum(gathered.astype(jnp.float32), axis=1).astype(jnp.bfloat16)
    expert_out = expert_out.reshape(dp_size, capacity, slice_width)
    returned = lax.all_to_all(expert_out, "dp", split_axis=0, concat_axis=0, tiled=True)
    picked = jnp.take(returned.reshape(experts * capacity, slice_width), slot_ids, axis=0)
    picked = picked.reshape(token_count, top_count, slice_width)
    shares = route_weights.astype(jnp.float32)
    shares = shares / jnp.sum(shares, axis=1, keepdims=True)
    mix_cols = jnp.einsum("tk,tkd->td", shares, picked.astype(jnp.float32)).astype(jnp.bfloat16)
    expert_mix = lax.all_gather(mix_cols, "tp", axis=1, tiled=True)
    attended = attend_local(
        queries, key_codes, key_scales, cache_values, new_keys, new_values, lengths
    )
    return (expert_mix, attended)


def solution(mesh):
    placed = (
        P("dp", None),
        P("dp", None),
        P("dp", None),
        P("dp", None, "tp"),
        P("dp", None, "tp"),
        P("dp", "tp", None),
        P("dp", "tp"),
        P("dp", "tp"),
        P("tp", "dp"),
        P("dp", "tp"),
        P("dp", "tp"),
        P("dp", "tp"),
        P("dp"),
    )
    return jax.shard_map(
        on_device,
        mesh=mesh,
        in_specs=placed,
        out_specs=(P("dp", None), P("dp", "tp")),
        check_vma=False,
    )
```

```python
import jax
import jax.numpy as jnp
from jax import lax
from jax.sharding import PartitionSpec as P

rope_base = 1000000.0


def inverse_freq(head_size):
    steps = jnp.arange(head_size // 2, dtype=jnp.float32) * (2.0 / head_size)
    return jnp.exp(-steps * jnp.log(jnp.float32(rope_base)))


def rotate(vector, angles):
    half_size = vector.shape[-1] // 2
    front_half = vector[..., :half_size]
    back_half = vector[..., half_size:]
    cosine = jnp.cos(angles)
    sine_part = jnp.sin(angles)
    return jnp.concatenate(
        [front_half * cosine - back_half * sine_part, back_half * cosine + front_half * sine_part],
        axis=-1,
    )


def attend_local(queries, codes, scales, cache_values, new_keys, new_values, lengths):
    row_count = queries.shape[0]
    cache_len = codes.shape[0]
    groups = scales.shape[0]
    head_size = codes.shape[1] // groups
    per_group = queries.shape[1] // (groups * head_size)
    request_end = jnp.cumsum(lengths)
    starts = request_end - lengths
    cache_pos = jnp.arange(cache_len, dtype=jnp.int32)
    member = (cache_pos[:, None] >= starts[None, :]) & (cache_pos[:, None] < request_end[None, :])
    offset = jnp.sum(jnp.where(member, starts[None, :], 0), axis=1)
    position = (cache_pos - offset).astype(jnp.float32)
    frequency = inverse_freq(head_size)
    cache_keys = (
        codes.astype(jnp.float32).reshape(cache_len, groups, head_size)
        * jnp.transpose(scales)[:, :, None]
    )
    cache_keys = rotate(cache_keys, position[:, None, None] * frequency[None, None, :]).astype(
        jnp.bfloat16
    )
    query_angles = lengths.astype(jnp.float32)[:, None] * frequency[None, :]
    rotated_query = queries.astype(jnp.float32).reshape(row_count, groups, per_group, head_size)
    rotated_query = rotate(rotated_query, query_angles[:, None, None, :]).astype(jnp.bfloat16)
    fresh_key = rotate(
        new_keys.astype(jnp.float32).reshape(row_count, groups, head_size), query_angles[:, None, :]
    ).astype(jnp.bfloat16)
    score_scale = head_size ** (-0.5)
    scores = (
        jnp.einsum("rgqd,cgd->rgqc", rotated_query, cache_keys, preferred_element_type=jnp.float32)
        * score_scale
    )
    own_score = (
        jnp.einsum("rgqd,rgd->rgq", rotated_query, fresh_key, preferred_element_type=jnp.float32)
        * score_scale
    )
    live_mask = jnp.transpose(member)[:, None, None, :]
    scores = jnp.where(live_mask, scores, -jnp.inf)
    peak_score = jnp.maximum(jnp.max(scores, axis=-1), own_score)
    weights = jnp.exp(scores - peak_score[..., None])
    own_weight = jnp.exp(own_score - peak_score)
    weight_sum = jnp.sum(weights, axis=-1) + own_weight
    value_rows = cache_values.reshape(cache_len, groups, head_size)
    mixture = jnp.einsum(
        "rgqc,cgd->rgqd",
        weights.astype(jnp.bfloat16),
        value_rows,
        preferred_element_type=jnp.float32,
    )
    mixture = mixture + own_weight[..., None] * new_values.astype(jnp.float32).reshape(
        row_count, groups, 1, head_size
    )
    return (
        (mixture / weight_sum[..., None])
        .reshape(row_count, groups * per_group * head_size)
        .astype(jnp.bfloat16)
    )


def expert_block(arrived, w_gate, w_up, w_down):
    arrived_shape = arrived.shape
    inputs = arrived.reshape(-1, arrived_shape[-1])
    gate_act = jnp.dot(inputs, w_gate[0], preferred_element_type=jnp.float32)
    up_act = jnp.dot(inputs, w_up[0], preferred_element_type=jnp.float32)
    hidden_act = (jax.nn.silu(gate_act) * up_act).astype(jnp.bfloat16)
    partial_value = jnp.dot(hidden_act, w_down[0], preferred_element_type=jnp.float32)
    return partial_value.reshape(arrived_shape[0], arrived_shape[1], partial_value.shape[-1])


def on_device(
    hidden,
    routes,
    route_weights,
    w_gate,
    w_up,
    w_down,
    queries,
    key_codes,
    key_scales,
    cache_values,
    new_keys,
    new_values,
    lengths,
):
    token_count = routes.shape[0]
    top_count = routes.shape[1]
    model_width = hidden.shape[1]
    tp_size = lax.axis_size("tp")
    dp_size = lax.axis_size("dp")
    slice_width = model_width // tp_size
    experts = dp_size * w_gate.shape[0]
    capacity = min(token_count, max(2, token_count * top_count * 2 // experts))
    flat_ids = routes.reshape(-1)
    onehot = (flat_ids[:, None] == jnp.arange(experts, dtype=jnp.int32)[None, :]).astype(jnp.int32)
    rank_ids = jnp.sum(onehot * (jnp.cumsum(onehot, axis=0) - 1), axis=1)
    slot_ids = flat_ids * capacity + rank_ids
    slot_grid = slot_ids.reshape(token_count, top_count)
    selector = jnp.any(
        jnp.arange(experts * capacity, dtype=jnp.int32)[:, None, None] == slot_grid[None, :, :],
        axis=2,
    ).astype(jnp.bfloat16)
    outgoing = jnp.dot(selector, hidden, preferred_element_type=jnp.float32).astype(jnp.bfloat16)
    outgoing = outgoing.reshape(experts, capacity, model_width)
    arrived = lax.all_to_all(outgoing, "dp", split_axis=0, concat_axis=0, tiled=True)
    slots = dp_size * capacity
    arrived = arrived.reshape(slots, model_width)
    gate_act = jnp.dot(arrived, w_gate[0], preferred_element_type=jnp.float32)
    up_act = jnp.dot(arrived, w_up[0], preferred_element_type=jnp.float32)
    hidden_act = (jax.nn.silu(gate_act) * up_act).astype(jnp.bfloat16)
    down_w = w_down[0].reshape(w_down.shape[1], tp_size, slice_width)
    partial_value = jnp.einsum("sh,hcd->csd", hidden_act, down_w, preferred_element_type=jnp.float32)
    partial_value = partial_value.astype(jnp.bfloat16)
    gathered = lax.all_to_all(partial_value, "tp", split_axis=0, concat_axis=0, tiled=True)
    expert_out = jnp.sum(gathered.astype(jnp.float32), axis=0).astype(jnp.bfloat16)
    expert_out = expert_out.reshape(dp_size, capacity, slice_width)
    returned = lax.all_to_all(expert_out, "dp", split_axis=0, concat_axis=0, tiled=True)
    picked = jnp.take(returned.reshape(experts * capacity, slice_width), slot_ids, axis=0)
    picked = picked.reshape(token_count, top_count, slice_width)
    shares = route_weights.astype(jnp.float32)
    shares = shares / jnp.sum(shares, axis=1, keepdims=True)
    mix_cols = jnp.einsum("tk,tkd->td", shares, picked.astype(jnp.float32)).astype(jnp.bfloat16)
    expert_mix = lax.all_gather(mix_cols, "tp", axis=1, tiled=True)
    attended = attend_local(
        queries, key_codes, key_scales, cache_values, new_keys, new_values, lengths
    )
    return (expert_mix, attended)


def solution(mesh):
    placed = (
        P("dp", None),
        P("dp", None),
        P("dp", None),
        P("dp", None, "tp"),
        P("dp", None, "tp"),
        P("dp", "tp", None),
        P("dp", "tp"),
        P("dp", "tp"),
        P("tp", "dp"),
        P("dp", "tp"),
        P("dp", "tp"),
        P("dp", "tp"),
        P("dp"),
    )
    return jax.shard_map(
        on_device,
        mesh=mesh,
        in_specs=placed,
        out_specs=(P("dp", None), P("dp", "tp")),
        check_vma=False,
    )
```

```python
import jax
import jax.numpy as jnp
from jax import lax
from jax.sharding import PartitionSpec as P

rope_base = 1000000.0


def inverse_freq(head_size):
    steps = jnp.arange(head_size // 2, dtype=jnp.float32) * (2.0 / head_size)
    return jnp.exp(-steps * jnp.log(jnp.float32(rope_base)))


def rotate(vector, angles):
    half_size = vector.shape[-1] // 2
    front_half = vector[..., :half_size]
    back_half = vector[..., half_size:]
    cosine = jnp.cos(angles)
    sine_part = jnp.sin(angles)
    return jnp.concatenate(
        [front_half * cosine - back_half * sine_part, back_half * cosine + front_half * sine_part],
        axis=-1,
    )


def attend_local(queries, codes, scales, cache_values, new_keys, new_values, lengths):
    row_count = queries.shape[0]
    cache_len = codes.shape[0]
    groups = scales.shape[0]
    head_size = codes.shape[1] // groups
    per_group = queries.shape[1] // (groups * head_size)
    request_end = jnp.cumsum(lengths)
    starts = request_end - lengths
    cache_pos = jnp.arange(cache_len, dtype=jnp.int32)
    member = (cache_pos[:, None] >= starts[None, :]) & (cache_pos[:, None] < request_end[None, :])
    offset = jnp.sum(jnp.where(member, starts[None, :], 0), axis=1)
    position = (cache_pos - offset).astype(jnp.float32)
    frequency = inverse_freq(head_size)
    cache_keys = (
        codes.astype(jnp.float32).reshape(cache_len, groups, head_size)
        * jnp.transpose(scales)[:, :, None]
    )
    cache_keys = rotate(cache_keys, position[:, None, None] * frequency[None, None, :]).astype(
        jnp.bfloat16
    )
    query_angles = lengths.astype(jnp.float32)[:, None] * frequency[None, :]
    rotated_query = queries.astype(jnp.float32).reshape(row_count, groups, per_group, head_size)
    rotated_query = rotate(rotated_query, query_angles[:, None, None, :]).astype(jnp.bfloat16)
    fresh_key = rotate(
        new_keys.astype(jnp.float32).reshape(row_count, groups, head_size), query_angles[:, None, :]
    ).astype(jnp.bfloat16)
    score_scale = head_size ** (-0.5)
    scores = (
        jnp.einsum("rgqd,cgd->rgqc", rotated_query, cache_keys, preferred_element_type=jnp.float32)
        * score_scale
    )
    own_score = (
        jnp.einsum("rgqd,rgd->rgq", rotated_query, fresh_key, preferred_element_type=jnp.float32)
        * score_scale
    )
    live_mask = jnp.transpose(member)[:, None, None, :]
    scores = jnp.where(live_mask, scores, -jnp.inf)
    peak_score = jnp.maximum(jnp.max(scores, axis=-1), own_score)
    weights = jnp.exp(scores - peak_score[..., None])
    own_weight = jnp.exp(own_score - peak_score)
    weight_sum = jnp.sum(weights, axis=-1) + own_weight
    value_rows = cache_values.reshape(cache_len, groups, head_size)
    mixture = jnp.einsum(
        "rgqc,cgd->rgqd",
        weights.astype(jnp.bfloat16),
        value_rows,
        preferred_element_type=jnp.float32,
    )
    mixture = mixture + own_weight[..., None] * new_values.astype(jnp.float32).reshape(
        row_count, groups, 1, head_size
    )
    return (
        (mixture / weight_sum[..., None])
        .reshape(row_count, groups * per_group * head_size)
        .astype(jnp.bfloat16)
    )


def expert_block(arrived, w_gate, w_up, w_down):
    arrived_shape = arrived.shape
    inputs = arrived.reshape(-1, arrived_shape[-1])
    gate_act = jnp.dot(inputs, w_gate[0], preferred_element_type=jnp.float32)
    up_act = jnp.dot(inputs, w_up[0], preferred_element_type=jnp.float32)
    hidden_act = (jax.nn.silu(gate_act) * up_act).astype(jnp.bfloat16)
    partial_value = jnp.dot(hidden_act, w_down[0], preferred_element_type=jnp.float32)
    return partial_value.reshape(arrived_shape[0], arrived_shape[1], partial_value.shape[-1])


def on_device(
    hidden,
    routes,
    route_weights,
    w_gate,
    w_up,
    w_down,
    queries,
    key_codes,
    key_scales,
    cache_values,
    new_keys,
    new_values,
    lengths,
):
    token_count = routes.shape[0]
    top_count = routes.shape[1]
    model_width = hidden.shape[1]
    tp_size = lax.axis_size("tp")
    dp_size = lax.axis_size("dp")
    slice_width = model_width // tp_size
    experts = dp_size * w_gate.shape[0]
    capacity = min(token_count, max(2, token_count * top_count * 2 // experts))
    flat_ids = routes.reshape(-1)
    pair_count = flat_ids.shape[0]
    pair_pos = jnp.arange(pair_count, dtype=jnp.int32)
    same_before = (flat_ids[:, None] == flat_ids[None, :]) & (pair_pos[None, :] < pair_pos[:, None])
    rank_ids = jnp.sum(same_before.astype(jnp.int32), axis=1)
    slot_ids = flat_ids * capacity + rank_ids
    slot_pos = jnp.arange(experts * capacity, dtype=jnp.int32)
    slot_hit = slot_pos[:, None] == slot_ids[None, :]
    slot_token = jnp.sum(jnp.where(slot_hit, pair_pos[None, :] // top_count, 0), axis=1)
    slot_token = jnp.where(jnp.any(slot_hit, axis=1), slot_token, token_count)
    padded = jnp.concatenate([hidden, jnp.zeros((1, model_width), hidden.dtype)], axis=0)
    outgoing = padded[slot_token.reshape(experts, capacity)]
    arrived = lax.all_to_all(outgoing, "dp", split_axis=0, concat_axis=0, tiled=True)
    slots = dp_size * capacity
    gate_act = jnp.einsum("ecd,dh->ech", arrived, w_gate[0], preferred_element_type=jnp.float32)
    up_act = jnp.einsum("ecd,dh->ech", arrived, w_up[0], preferred_element_type=jnp.float32)
    hidden_act = (jax.nn.silu(gate_act) * up_act).astype(jnp.bfloat16).reshape(slots, -1)
    down_w = w_down[0].reshape(w_down.shape[1], tp_size, slice_width)
    partial_value = jnp.einsum("sh,hcd->csd", hidden_act, down_w, preferred_element_type=jnp.float32)
    partial_value = partial_value.astype(jnp.bfloat16)
    gathered = lax.all_to_all(partial_value, "tp", split_axis=0, concat_axis=0, tiled=True)
    expert_out = jnp.sum(gathered.astype(jnp.float32), axis=0).astype(jnp.bfloat16)
    expert_out = expert_out.reshape(dp_size, capacity, slice_width)
    returned = lax.all_to_all(expert_out, "dp", split_axis=0, concat_axis=0, tiled=True)
    picked = jnp.take(returned.reshape(experts * capacity, slice_width), slot_ids, axis=0)
    picked = picked.reshape(token_count, top_count, slice_width)
    shares = route_weights.astype(jnp.float32)
    shares = shares / jnp.sum(shares, axis=1, keepdims=True)
    mix_cols = jnp.einsum("tk,tkd->td", shares, picked.astype(jnp.float32)).astype(jnp.bfloat16)
    spread = jnp.broadcast_to(mix_cols[:, None, :], (token_count, tp_size, slice_width))
    expert_mix = lax.all_to_all(spread, "tp", split_axis=1, concat_axis=1, tiled=True)
    expert_mix = expert_mix.reshape(token_count, model_width)
    attended = attend_local(
        queries, key_codes, key_scales, cache_values, new_keys, new_values, lengths
    )
    return (expert_mix, attended)


def solution(mesh):
    placed = (
        P("dp", None),
        P("dp", None),
        P("dp", None),
        P("dp", None, "tp"),
        P("dp", None, "tp"),
        P("dp", "tp", None),
        P("dp", "tp"),
        P("dp", "tp"),
        P("tp", "dp"),
        P("dp", "tp"),
        P("dp", "tp"),
        P("dp", "tp"),
        P("dp"),
    )
    return jax.shard_map(
        on_device,
        mesh=mesh,
        in_specs=placed,
        out_specs=(P("dp", None), P("dp", "tp")),
        check_vma=False,
    )
```

```python
import jax
import jax.numpy as jnp
from jax import lax
from jax.sharding import PartitionSpec as P

rope_base = 1000000.0


def inverse_freq(head_size):
    steps = jnp.arange(head_size // 2, dtype=jnp.float32) * (2.0 / head_size)
    return jnp.exp(-steps * jnp.log(jnp.float32(rope_base)))


def rotate(vector, angles):
    half_size = vector.shape[-1] // 2
    front_half = vector[..., :half_size]
    back_half = vector[..., half_size:]
    cosine = jnp.cos(angles)
    sine_part = jnp.sin(angles)
    return jnp.concatenate(
        [front_half * cosine - back_half * sine_part, back_half * cosine + front_half * sine_part],
        axis=-1,
    )


def attend_local(queries, codes, scales, cache_values, new_keys, new_values, lengths):
    row_count = queries.shape[0]
    cache_len = codes.shape[0]
    groups = scales.shape[0]
    head_size = codes.shape[1] // groups
    per_group = queries.shape[1] // (groups * head_size)
    request_end = jnp.cumsum(lengths)
    starts = request_end - lengths
    cache_pos = jnp.arange(cache_len, dtype=jnp.int32)
    member = (cache_pos[:, None] >= starts[None, :]) & (cache_pos[:, None] < request_end[None, :])
    offset = jnp.sum(jnp.where(member, starts[None, :], 0), axis=1)
    position = (cache_pos - offset).astype(jnp.float32)
    frequency = inverse_freq(head_size)
    cache_keys = (
        codes.astype(jnp.float32).reshape(cache_len, groups, head_size)
        * jnp.transpose(scales)[:, :, None]
    )
    cache_keys = rotate(cache_keys, position[:, None, None] * frequency[None, None, :]).astype(
        jnp.bfloat16
    )
    query_angles = lengths.astype(jnp.float32)[:, None] * frequency[None, :]
    rotated_query = queries.astype(jnp.float32).reshape(row_count, groups, per_group, head_size)
    rotated_query = rotate(rotated_query, query_angles[:, None, None, :]).astype(jnp.bfloat16)
    fresh_key = rotate(
        new_keys.astype(jnp.float32).reshape(row_count, groups, head_size), query_angles[:, None, :]
    ).astype(jnp.bfloat16)
    score_scale = head_size ** (-0.5)
    scores = (
        jnp.einsum("rgqd,cgd->rgqc", rotated_query, cache_keys, preferred_element_type=jnp.float32)
        * score_scale
    )
    own_score = (
        jnp.einsum("rgqd,rgd->rgq", rotated_query, fresh_key, preferred_element_type=jnp.float32)
        * score_scale
    )
    live_mask = jnp.transpose(member)[:, None, None, :]
    scores = jnp.where(live_mask, scores, -jnp.inf)
    peak_score = jnp.maximum(jnp.max(scores, axis=-1), own_score)
    weights = jnp.exp(scores - peak_score[..., None])
    own_weight = jnp.exp(own_score - peak_score)
    weight_sum = jnp.sum(weights, axis=-1) + own_weight
    value_rows = cache_values.reshape(cache_len, groups, head_size)
    mixture = jnp.einsum(
        "rgqc,cgd->rgqd",
        weights.astype(jnp.bfloat16),
        value_rows,
        preferred_element_type=jnp.float32,
    )
    mixture = mixture + own_weight[..., None] * new_values.astype(jnp.float32).reshape(
        row_count, groups, 1, head_size
    )
    return (
        (mixture / weight_sum[..., None])
        .reshape(row_count, groups * per_group * head_size)
        .astype(jnp.bfloat16)
    )


def expert_block(arrived, w_gate, w_up, w_down):
    arrived_shape = arrived.shape
    inputs = arrived.reshape(-1, arrived_shape[-1])
    gate_act = jnp.dot(inputs, w_gate[0], preferred_element_type=jnp.float32)
    up_act = jnp.dot(inputs, w_up[0], preferred_element_type=jnp.float32)
    hidden_act = (jax.nn.silu(gate_act) * up_act).astype(jnp.bfloat16)
    partial_value = jnp.dot(hidden_act, w_down[0], preferred_element_type=jnp.float32)
    return partial_value.reshape(arrived_shape[0], arrived_shape[1], partial_value.shape[-1])


def on_device(
    hidden,
    routes,
    route_weights,
    w_gate,
    w_up,
    w_down,
    queries,
    key_codes,
    key_scales,
    cache_values,
    new_keys,
    new_values,
    lengths,
):
    token_count = routes.shape[0]
    top_count = routes.shape[1]
    model_width = hidden.shape[1]
    tp_size = lax.axis_size("tp")
    dp_size = lax.axis_size("dp")
    slice_width = model_width // tp_size
    experts = dp_size * w_gate.shape[0]
    capacity = min(token_count, max(2, token_count * top_count * 2 // experts))
    flat_ids = routes.reshape(-1)
    pair_count = flat_ids.shape[0]
    pair_pos = jnp.arange(pair_count, dtype=jnp.int32)
    same_before = (flat_ids[:, None] == flat_ids[None, :]) & (pair_pos[None, :] < pair_pos[:, None])
    rank_ids = jnp.sum(same_before.astype(jnp.int32), axis=1)
    slot_ids = flat_ids * capacity + rank_ids
    slot_pos = jnp.arange(experts * capacity, dtype=jnp.int32)
    token_of_pair = pair_pos // top_count
    token_pos = jnp.arange(token_count, dtype=jnp.int32)
    slot_hit = slot_pos[:, None] == slot_ids[None, :]
    slot_token = jnp.sum(jnp.where(slot_hit, token_of_pair[None, :], 0), axis=1)
    slot_token = jnp.where(jnp.any(slot_hit, axis=1), slot_token, token_count)
    selector = (slot_token[:, None] == token_pos[None, :]).astype(hidden.dtype)
    selector = selector.reshape(experts, capacity, token_count)
    outgoing = jnp.einsum(
        "ect,td->ecd", selector, hidden, preferred_element_type=jnp.float32
    ).astype(hidden.dtype)
    arrived = lax.all_to_all(outgoing, "dp", split_axis=0, concat_axis=0, tiled=True)
    slots = dp_size * capacity
    gate_act = jnp.einsum("ecd,dh->ech", arrived, w_gate[0], preferred_element_type=jnp.float32)
    up_act = jnp.einsum("ecd,dh->ech", arrived, w_up[0], preferred_element_type=jnp.float32)
    hidden_act = (jax.nn.silu(gate_act) * up_act).astype(jnp.bfloat16).reshape(slots, -1)
    down_w = w_down[0].reshape(w_down.shape[1], tp_size, slice_width)
    partial_value = jnp.einsum("sh,hcd->csd", hidden_act, down_w, preferred_element_type=jnp.float32)
    partial_value = partial_value.astype(jnp.bfloat16)
    gathered = lax.all_to_all(partial_value, "tp", split_axis=0, concat_axis=0, tiled=True)
    expert_out = jnp.sum(gathered.astype(jnp.float32), axis=0).astype(jnp.bfloat16)
    expert_out = expert_out.reshape(dp_size, capacity, slice_width)
    returned = lax.all_to_all(expert_out, "dp", split_axis=0, concat_axis=0, tiled=True)
    picked = jnp.take(returned.reshape(experts * capacity, slice_width), slot_ids, axis=0)
    picked = picked.reshape(token_count, top_count, slice_width)
    shares = route_weights.astype(jnp.float32)
    shares = shares / jnp.sum(shares, axis=1, keepdims=True)
    mix_cols = jnp.einsum("tk,tkd->td", shares, picked.astype(jnp.float32)).astype(jnp.bfloat16)
    spread = jnp.broadcast_to(mix_cols[:, None, :], (token_count, tp_size, slice_width))
    expert_mix = lax.all_to_all(spread, "tp", split_axis=1, concat_axis=1, tiled=True)
    expert_mix = expert_mix.reshape(token_count, model_width)
    attended = attend_local(
        queries, key_codes, key_scales, cache_values, new_keys, new_values, lengths
    )
    return (expert_mix, attended)


def solution(mesh):
    placed = (
        P("dp", None),
        P("dp", None),
        P("dp", None),
        P("dp", None, "tp"),
        P("dp", None, "tp"),
        P("dp", "tp", None),
        P("dp", "tp"),
        P("dp", "tp"),
        P("tp", "dp"),
        P("dp", "tp"),
        P("dp", "tp"),
        P("dp", "tp"),
        P("dp"),
    )
    return jax.shard_map(
        on_device,
        mesh=mesh,
        in_specs=placed,
        out_specs=(P("dp", None), P("dp", "tp")),
        check_vma=False,
    )
```

```python
import jax
import jax.numpy as jnp
from jax import lax
from jax.sharding import PartitionSpec as P

rope_base = 1000000.0


def inverse_freq(head_size):
    steps = jnp.arange(head_size // 2, dtype=jnp.float32) * (2.0 / head_size)
    return jnp.exp(-steps * jnp.log(jnp.float32(rope_base)))


def rotate(vector, angles):
    half_size = vector.shape[-1] // 2
    front_half = vector[..., :half_size]
    back_half = vector[..., half_size:]
    cosine = jnp.cos(angles)
    sine_part = jnp.sin(angles)
    return jnp.concatenate(
        [front_half * cosine - back_half * sine_part, back_half * cosine + front_half * sine_part],
        axis=-1,
    )


def attend_local(queries, codes, scales, cache_values, new_keys, new_values, lengths):
    row_count = queries.shape[0]
    cache_len = codes.shape[0]
    groups = scales.shape[0]
    head_size = codes.shape[1] // groups
    per_group = queries.shape[1] // (groups * head_size)
    request_end = jnp.cumsum(lengths)
    starts = request_end - lengths
    cache_pos = jnp.arange(cache_len, dtype=jnp.int32)
    member = (cache_pos[:, None] >= starts[None, :]) & (cache_pos[:, None] < request_end[None, :])
    offset = jnp.sum(jnp.where(member, starts[None, :], 0), axis=1)
    position = (cache_pos - offset).astype(jnp.float32)
    frequency = inverse_freq(head_size)
    cache_keys = (
        codes.astype(jnp.float32).reshape(cache_len, groups, head_size)
        * jnp.transpose(scales)[:, :, None]
    )
    cache_keys = rotate(cache_keys, position[:, None, None] * frequency[None, None, :]).astype(
        jnp.bfloat16
    )
    query_angles = lengths.astype(jnp.float32)[:, None] * frequency[None, :]
    rotated_query = queries.astype(jnp.float32).reshape(row_count, groups, per_group, head_size)
    rotated_query = rotate(rotated_query, query_angles[:, None, None, :]).astype(jnp.bfloat16)
    fresh_key = rotate(
        new_keys.astype(jnp.float32).reshape(row_count, groups, head_size), query_angles[:, None, :]
    ).astype(jnp.bfloat16)
    score_scale = head_size ** (-0.5)
    scores = (
        jnp.einsum("rgqd,cgd->rgqc", rotated_query, cache_keys, preferred_element_type=jnp.float32)
        * score_scale
    )
    own_score = (
        jnp.einsum("rgqd,rgd->rgq", rotated_query, fresh_key, preferred_element_type=jnp.float32)
        * score_scale
    )
    live_mask = jnp.transpose(member)[:, None, None, :]
    scores = jnp.where(live_mask, scores, -jnp.inf)
    peak_score = jnp.maximum(jnp.max(scores, axis=-1), own_score)
    weights = jnp.exp(scores - peak_score[..., None])
    own_weight = jnp.exp(own_score - peak_score)
    weight_sum = jnp.sum(weights, axis=-1) + own_weight
    value_rows = cache_values.reshape(cache_len, groups, head_size)
    mixture = jnp.einsum(
        "rgqc,cgd->rgqd",
        weights.astype(jnp.bfloat16),
        value_rows,
        preferred_element_type=jnp.float32,
    )
    mixture = mixture + own_weight[..., None] * new_values.astype(jnp.float32).reshape(
        row_count, groups, 1, head_size
    )
    return (
        (mixture / weight_sum[..., None])
        .reshape(row_count, groups * per_group * head_size)
        .astype(jnp.bfloat16)
    )


def expert_block(arrived, w_gate, w_up, w_down):
    arrived_shape = arrived.shape
    inputs = arrived.reshape(-1, arrived_shape[-1])
    gate_act = jnp.dot(inputs, w_gate[0], preferred_element_type=jnp.float32)
    up_act = jnp.dot(inputs, w_up[0], preferred_element_type=jnp.float32)
    hidden_act = (jax.nn.silu(gate_act) * up_act).astype(jnp.bfloat16)
    partial_value = jnp.dot(hidden_act, w_down[0], preferred_element_type=jnp.float32)
    return partial_value.reshape(arrived_shape[0], arrived_shape[1], partial_value.shape[-1])


def on_device(
    hidden,
    routes,
    route_weights,
    w_gate,
    w_up,
    w_down,
    queries,
    key_codes,
    key_scales,
    cache_values,
    new_keys,
    new_values,
    lengths,
):
    token_count = routes.shape[0]
    top_count = routes.shape[1]
    model_width = hidden.shape[1]
    tp_size = lax.axis_size("tp")
    dp_size = lax.axis_size("dp")
    slice_width = model_width // tp_size
    experts = dp_size * w_gate.shape[0]
    capacity = min(token_count, max(2, token_count * top_count * 2 // experts))
    flat_ids = routes.reshape(-1)
    pair_count = flat_ids.shape[0]
    pair_pos = jnp.arange(pair_count, dtype=jnp.int32)
    same_before = (flat_ids[:, None] == flat_ids[None, :]) & (pair_pos[None, :] < pair_pos[:, None])
    rank_ids = jnp.sum(same_before.astype(jnp.int32), axis=1)
    slot_ids = flat_ids * capacity + rank_ids
    slot_pos = jnp.arange(experts * capacity, dtype=jnp.int32)
    token_of_pair = pair_pos // top_count
    token_pos = jnp.arange(token_count, dtype=jnp.int32)
    slot_hit = slot_pos[:, None] == slot_ids[None, :]
    slot_token = jnp.sum(jnp.where(slot_hit, token_of_pair[None, :], 0), axis=1)
    slot_token = jnp.where(jnp.any(slot_hit, axis=1), slot_token, token_count)
    selector = (slot_token[:, None] == token_pos[None, :]).astype(hidden.dtype)
    outgoing = jnp.dot(selector, hidden, preferred_element_type=jnp.float32).astype(hidden.dtype)
    outgoing = outgoing.reshape(experts, capacity, model_width)
    arrived = lax.all_to_all(outgoing, "dp", split_axis=0, concat_axis=0, tiled=True)
    slots = dp_size * capacity
    gate_act = jnp.einsum("ecd,dh->ech", arrived, w_gate[0], preferred_element_type=jnp.float32)
    up_act = jnp.einsum("ecd,dh->ech", arrived, w_up[0], preferred_element_type=jnp.float32)
    hidden_act = (jax.nn.silu(gate_act) * up_act).astype(jnp.bfloat16).reshape(slots, -1)
    down_w = w_down[0].reshape(w_down.shape[1], tp_size, slice_width)
    partial_value = jnp.einsum("sh,hcd->csd", hidden_act, down_w, preferred_element_type=jnp.float32)
    partial_value = partial_value.astype(jnp.bfloat16)
    gathered = lax.all_to_all(partial_value, "tp", split_axis=0, concat_axis=0, tiled=True)
    expert_out = jnp.sum(gathered.astype(jnp.float32), axis=0).astype(jnp.bfloat16)
    expert_out = expert_out.reshape(dp_size, capacity, slice_width)
    returned = lax.all_to_all(expert_out, "dp", split_axis=0, concat_axis=0, tiled=True)
    shares = route_weights.astype(jnp.float32)
    shares = shares / jnp.sum(shares, axis=1, keepdims=True)
    slot_grid = slot_ids.reshape(token_count, top_count)
    slot_weight = jnp.sum(
        jnp.where(slot_grid[:, :, None] == slot_pos[None, None, :], shares[:, :, None], 0.0), axis=1
    )
    mix_cols = jnp.dot(
        slot_weight,
        returned.reshape(experts * capacity, slice_width).astype(jnp.float32),
        precision=lax.Precision.HIGHEST,
        preferred_element_type=jnp.float32,
    ).astype(jnp.bfloat16)
    spread = jnp.broadcast_to(mix_cols[:, None, :], (token_count, tp_size, slice_width))
    expert_mix = lax.all_to_all(spread, "tp", split_axis=1, concat_axis=1, tiled=True)
    expert_mix = expert_mix.reshape(token_count, model_width)
    attended = attend_local(
        queries, key_codes, key_scales, cache_values, new_keys, new_values, lengths
    )
    return (expert_mix, attended)


def solution(mesh):
    placed = (
        P("dp", None),
        P("dp", None),
        P("dp", None),
        P("dp", None, "tp"),
        P("dp", None, "tp"),
        P("dp", "tp", None),
        P("dp", "tp"),
        P("dp", "tp"),
        P("tp", "dp"),
        P("dp", "tp"),
        P("dp", "tp"),
        P("dp", "tp"),
        P("dp"),
    )
    return jax.shard_map(
        on_device,
        mesh=mesh,
        in_specs=placed,
        out_specs=(P("dp", None), P("dp", "tp")),
        check_vma=False,
    )
```

```python
import jax
import jax.numpy as jnp
from jax import lax
from jax.sharding import PartitionSpec as P

rope_base = 1000000.0


def inverse_freq(head_size):
    steps = jnp.arange(head_size // 2, dtype=jnp.float32) * (2.0 / head_size)
    return jnp.exp(-steps * jnp.log(jnp.float32(rope_base)))


def rotate(vector, angles):
    half_size = vector.shape[-1] // 2
    front_half = vector[..., :half_size]
    back_half = vector[..., half_size:]
    cosine = jnp.cos(angles)
    sine_part = jnp.sin(angles)
    return jnp.concatenate(
        [front_half * cosine - back_half * sine_part, back_half * cosine + front_half * sine_part],
        axis=-1,
    )


def attend_local(queries, codes, scales, cache_values, new_keys, new_values, lengths):
    row_count = queries.shape[0]
    cache_len = codes.shape[0]
    groups = scales.shape[0]
    head_size = codes.shape[1] // groups
    per_group = queries.shape[1] // (groups * head_size)
    request_end = jnp.cumsum(lengths)
    starts = request_end - lengths
    cache_pos = jnp.arange(cache_len, dtype=jnp.int32)
    member = (cache_pos[:, None] >= starts[None, :]) & (cache_pos[:, None] < request_end[None, :])
    offset = jnp.sum(jnp.where(member, starts[None, :], 0), axis=1)
    position = (cache_pos - offset).astype(jnp.float32)
    frequency = inverse_freq(head_size)
    cache_keys = (
        codes.astype(jnp.float32).reshape(cache_len, groups, head_size)
        * jnp.transpose(scales)[:, :, None]
    )
    cache_keys = rotate(cache_keys, position[:, None, None] * frequency[None, None, :]).astype(
        jnp.bfloat16
    )
    query_angles = lengths.astype(jnp.float32)[:, None] * frequency[None, :]
    rotated_query = queries.astype(jnp.float32).reshape(row_count, groups, per_group, head_size)
    rotated_query = rotate(rotated_query, query_angles[:, None, None, :]).astype(jnp.bfloat16)
    fresh_key = rotate(
        new_keys.astype(jnp.float32).reshape(row_count, groups, head_size), query_angles[:, None, :]
    ).astype(jnp.bfloat16)
    score_scale = head_size ** (-0.5)
    scores = (
        jnp.einsum("rgqd,cgd->rgqc", rotated_query, cache_keys, preferred_element_type=jnp.float32)
        * score_scale
    )
    own_score = (
        jnp.einsum("rgqd,rgd->rgq", rotated_query, fresh_key, preferred_element_type=jnp.float32)
        * score_scale
    )
    live_mask = jnp.transpose(member)[:, None, None, :]
    scores = jnp.where(live_mask, scores, -jnp.inf)
    peak_score = jnp.maximum(jnp.max(scores, axis=-1), own_score)
    weights = jnp.exp(scores - peak_score[..., None])
    own_weight = jnp.exp(own_score - peak_score)
    weight_sum = jnp.sum(weights, axis=-1) + own_weight
    value_rows = cache_values.reshape(cache_len, groups, head_size)
    mixture = jnp.einsum(
        "rgqc,cgd->rgqd",
        weights.astype(jnp.bfloat16),
        value_rows,
        preferred_element_type=jnp.float32,
    )
    mixture = mixture + own_weight[..., None] * new_values.astype(jnp.float32).reshape(
        row_count, groups, 1, head_size
    )
    return (
        (mixture / weight_sum[..., None])
        .reshape(row_count, groups * per_group * head_size)
        .astype(jnp.bfloat16)
    )


def expert_block(arrived, w_gate, w_up, w_down):
    arrived_shape = arrived.shape
    inputs = arrived.reshape(-1, arrived_shape[-1])
    gate_act = jnp.dot(inputs, w_gate[0], preferred_element_type=jnp.float32)
    up_act = jnp.dot(inputs, w_up[0], preferred_element_type=jnp.float32)
    hidden_act = (jax.nn.silu(gate_act) * up_act).astype(jnp.bfloat16)
    partial_value = jnp.dot(hidden_act, w_down[0], preferred_element_type=jnp.float32)
    return partial_value.reshape(arrived_shape[0], arrived_shape[1], partial_value.shape[-1])


def on_device(
    hidden,
    routes,
    route_weights,
    w_gate,
    w_up,
    w_down,
    queries,
    key_codes,
    key_scales,
    cache_values,
    new_keys,
    new_values,
    lengths,
):
    token_count = routes.shape[0]
    top_count = routes.shape[1]
    model_width = hidden.shape[1]
    tp_size = lax.axis_size("tp")
    dp_size = lax.axis_size("dp")
    slice_width = model_width // tp_size
    experts = dp_size * w_gate.shape[0]
    capacity = min(token_count, max(2, token_count * top_count * 2 // experts))
    flat_ids = routes.reshape(-1)
    pair_count = flat_ids.shape[0]
    pair_pos = jnp.arange(pair_count, dtype=jnp.int32)
    same_before = (flat_ids[:, None] == flat_ids[None, :]) & (pair_pos[None, :] < pair_pos[:, None])
    rank_ids = jnp.sum(same_before.astype(jnp.int32), axis=1)
    slot_ids = flat_ids * capacity + rank_ids
    slot_pos = jnp.arange(experts * capacity, dtype=jnp.int32)
    token_of_pair = pair_pos // top_count
    token_pos = jnp.arange(token_count, dtype=jnp.int32)
    slot_hit = slot_pos[:, None] == slot_ids[None, :]
    slot_token = jnp.sum(jnp.where(slot_hit, token_of_pair[None, :], 0), axis=1)
    slot_token = jnp.where(jnp.any(slot_hit, axis=1), slot_token, token_count)
    selector = (slot_token[:, None] == token_pos[None, :]).astype(hidden.dtype)
    outgoing = jnp.dot(selector, hidden, preferred_element_type=jnp.float32).astype(hidden.dtype)
    outgoing = outgoing.reshape(experts, capacity, model_width)
    arrived = lax.all_to_all(outgoing, "dp", split_axis=0, concat_axis=0, tiled=True)
    slots = dp_size * capacity
    gate_act = jnp.einsum("ecd,dh->ech", arrived, w_gate[0], preferred_element_type=jnp.float32)
    up_act = jnp.einsum("ecd,dh->ech", arrived, w_up[0], preferred_element_type=jnp.float32)
    hidden_act = (jax.nn.silu(gate_act) * up_act).astype(jnp.bfloat16).reshape(slots, -1)
    down_w = w_down[0].reshape(w_down.shape[1], tp_size, slice_width)
    partial_value = jnp.einsum("sh,hcd->csd", hidden_act, down_w, preferred_element_type=jnp.float32)
    partial_value = partial_value.astype(jnp.bfloat16)
    gathered = lax.all_to_all(partial_value, "tp", split_axis=0, concat_axis=0, tiled=True)
    gathered = gathered.reshape(tp_size, dp_size, capacity, slice_width)
    expert_out = jnp.sum(gathered.astype(jnp.float32), axis=0).astype(jnp.bfloat16)
    returned = lax.all_to_all(expert_out, "dp", split_axis=0, concat_axis=0, tiled=True)
    shares = route_weights.astype(jnp.float32)
    shares = shares / jnp.sum(shares, axis=1, keepdims=True)
    slot_grid = slot_ids.reshape(token_count, top_count)
    slot_weight = jnp.sum(
        jnp.where(slot_grid[:, :, None] == slot_pos[None, None, :], shares[:, :, None], 0.0), axis=1
    )
    slot_weight = jnp.broadcast_to(slot_weight[None], (tp_size,) + slot_weight.shape)
    spread = jnp.einsum(
        "cts,sd->ctd",
        slot_weight,
        returned.reshape(experts * capacity, slice_width).astype(jnp.float32),
        precision=lax.Precision.HIGHEST,
        preferred_element_type=jnp.float32,
    ).astype(jnp.bfloat16)
    expert_mix = lax.all_to_all(spread, "tp", split_axis=0, concat_axis=0, tiled=True)
    expert_mix = jnp.transpose(expert_mix, (1, 0, 2)).reshape(token_count, model_width)
    attended = attend_local(
        queries, key_codes, key_scales, cache_values, new_keys, new_values, lengths
    )
    return (expert_mix, attended)


def solution(mesh):
    placed = (
        P("dp", None),
        P("dp", None),
        P("dp", None),
        P("dp", None, "tp"),
        P("dp", None, "tp"),
        P("dp", "tp", None),
        P("dp", "tp"),
        P("dp", "tp"),
        P("tp", "dp"),
        P("dp", "tp"),
        P("dp", "tp"),
        P("dp", "tp"),
        P("dp"),
    )
    return jax.shard_map(
        on_device,
        mesh=mesh,
        in_specs=placed,
        out_specs=(P("dp", None), P("dp", "tp")),
        check_vma=False,
    )
```

```python
import jax
import jax.numpy as jnp
from jax import lax
from jax.sharding import PartitionSpec as P
from jax.experimental import pallas as pl
from jax.experimental.pallas import tpu as pltpu

rope_base = 1000000.0


def inverse_freq(head_size):
    steps = jnp.arange(head_size // 2, dtype=jnp.float32) * (2.0 / head_size)
    return jnp.exp(-steps * jnp.log(jnp.float32(rope_base)))


def rotate(vector, angles):
    half_size = vector.shape[-1] // 2
    front_half = vector[..., :half_size]
    back_half = vector[..., half_size:]
    cosine = jnp.cos(angles)
    sine_part = jnp.sin(angles)
    return jnp.concatenate(
        [front_half * cosine - back_half * sine_part, back_half * cosine + front_half * sine_part],
        axis=-1,
    )


def attend_local(queries, codes, scales, cache_values, new_keys, new_values, lengths):
    row_count = queries.shape[0]
    cache_len = codes.shape[0]
    groups = scales.shape[0]
    head_size = codes.shape[1] // groups
    per_group = queries.shape[1] // (groups * head_size)
    request_end = jnp.cumsum(lengths)
    starts = request_end - lengths
    cache_pos = jnp.arange(cache_len, dtype=jnp.int32)
    member = (cache_pos[:, None] >= starts[None, :]) & (cache_pos[:, None] < request_end[None, :])
    offset = jnp.sum(jnp.where(member, starts[None, :], 0), axis=1)
    position = (cache_pos - offset).astype(jnp.float32)
    frequency = inverse_freq(head_size)
    cache_keys = (
        codes.astype(jnp.float32).reshape(cache_len, groups, head_size)
        * jnp.transpose(scales)[:, :, None]
    )
    cache_keys = rotate(cache_keys, position[:, None, None] * frequency[None, None, :]).astype(
        jnp.bfloat16
    )
    query_angles = lengths.astype(jnp.float32)[:, None] * frequency[None, :]
    rotated_query = queries.astype(jnp.float32).reshape(row_count, groups, per_group, head_size)
    rotated_query = rotate(rotated_query, query_angles[:, None, None, :]).astype(jnp.bfloat16)
    fresh_key = rotate(
        new_keys.astype(jnp.float32).reshape(row_count, groups, head_size), query_angles[:, None, :]
    ).astype(jnp.bfloat16)
    score_scale = head_size ** (-0.5)
    scores = (
        jnp.einsum("rgqd,cgd->rgqc", rotated_query, cache_keys, preferred_element_type=jnp.float32)
        * score_scale
    )
    own_score = (
        jnp.einsum("rgqd,rgd->rgq", rotated_query, fresh_key, preferred_element_type=jnp.float32)
        * score_scale
    )
    live_mask = jnp.transpose(member)[:, None, None, :]
    scores = jnp.where(live_mask, scores, -jnp.inf)
    peak_score = jnp.maximum(jnp.max(scores, axis=-1), own_score)
    weights = jnp.exp(scores - peak_score[..., None])
    own_weight = jnp.exp(own_score - peak_score)
    weight_sum = jnp.sum(weights, axis=-1) + own_weight
    value_rows = cache_values.reshape(cache_len, groups, head_size)
    mixture = jnp.einsum(
        "rgqc,cgd->rgqd",
        weights.astype(jnp.bfloat16),
        value_rows,
        preferred_element_type=jnp.float32,
    )
    mixture = mixture + own_weight[..., None] * new_values.astype(jnp.float32).reshape(
        row_count, groups, 1, head_size
    )
    return (
        (mixture / weight_sum[..., None])
        .reshape(row_count, groups * per_group * head_size)
        .astype(jnp.bfloat16)
    )


def expert_kernel(x_ref, gate_ref, up_ref, down_ref, out_ref):
    inputs = x_ref[...]
    gate_act = jnp.dot(inputs, gate_ref[...], preferred_element_type=jnp.float32)
    up_act = jnp.dot(inputs, up_ref[...], preferred_element_type=jnp.float32)
    hidden_act = (gate_act / (1.0 + jnp.exp(-gate_act)) * up_act).astype(jnp.bfloat16)
    partial_value = jnp.dot(hidden_act, down_ref[...], preferred_element_type=jnp.float32)
    pieces = out_ref.shape[0]
    width = out_ref.shape[2]
    for piece in range(pieces):
        out_ref[piece] = partial_value[:, piece * width:(piece + 1) * width].astype(out_ref.dtype)


def expert_ffn(inputs, gate_w, up_w, down_w, pieces):
    rows = inputs.shape[0]
    width = down_w.shape[1] // pieces
    in_vmem = pl.BlockSpec(memory_space=pltpu.VMEM)
    return pl.pallas_call(
        expert_kernel,
        out_shape=jax.ShapeDtypeStruct((pieces, rows, width), jnp.bfloat16),
        in_specs=[in_vmem, in_vmem, in_vmem, in_vmem],
        out_specs=pl.BlockSpec(memory_space=pltpu.VMEM),
    )(inputs, gate_w, up_w, down_w)

def expert_block(arrived, w_gate, w_up, w_down):
    arrived_shape = arrived.shape
    inputs = arrived.reshape(-1, arrived_shape[-1])
    gate_act = jnp.dot(inputs, w_gate[0], preferred_element_type=jnp.float32)
    up_act = jnp.dot(inputs, w_up[0], preferred_element_type=jnp.float32)
    hidden_act = (jax.nn.silu(gate_act) * up_act).astype(jnp.bfloat16)
    partial_value = jnp.dot(hidden_act, w_down[0], preferred_element_type=jnp.float32)
    return partial_value.reshape(arrived_shape[0], arrived_shape[1], partial_value.shape[-1])


def on_device(
    hidden,
    routes,
    route_weights,
    w_gate,
    w_up,
    w_down,
    queries,
    key_codes,
    key_scales,
    cache_values,
    new_keys,
    new_values,
    lengths,
):
    token_count = routes.shape[0]
    top_count = routes.shape[1]
    model_width = hidden.shape[1]
    tp_size = lax.axis_size("tp")
    dp_size = lax.axis_size("dp")
    slice_width = model_width // tp_size
    experts = dp_size * w_gate.shape[0]
    capacity = min(token_count, max(2, token_count * top_count * 2 // experts))
    flat_ids = routes.reshape(-1)
    pair_count = flat_ids.shape[0]
    pair_pos = jnp.arange(pair_count, dtype=jnp.int32)
    same_before = (flat_ids[:, None] == flat_ids[None, :]) & (pair_pos[None, :] < pair_pos[:, None])
    rank_ids = jnp.sum(same_before.astype(jnp.int32), axis=1)
    slot_ids = flat_ids * capacity + rank_ids
    slot_pos = jnp.arange(experts * capacity, dtype=jnp.int32)
    token_of_pair = pair_pos // top_count
    token_pos = jnp.arange(token_count, dtype=jnp.int32)
    slot_hit = slot_pos[:, None] == slot_ids[None, :]
    slot_token = jnp.sum(jnp.where(slot_hit, token_of_pair[None, :], 0), axis=1)
    slot_token = jnp.where(jnp.any(slot_hit, axis=1), slot_token, token_count)
    selector = (slot_token[:, None] == token_pos[None, :]).astype(hidden.dtype)
    outgoing = jnp.dot(selector, hidden, preferred_element_type=jnp.float32).astype(hidden.dtype)
    outgoing = outgoing.reshape(experts, capacity, model_width)
    arrived = lax.all_to_all(outgoing, "dp", split_axis=0, concat_axis=0, tiled=True)
    slots = dp_size * capacity
    partial_value = expert_ffn(
        arrived.reshape(slots, model_width), w_gate[0], w_up[0], w_down[0], tp_size
    )
    gathered = lax.all_to_all(partial_value, "tp", split_axis=0, concat_axis=0, tiled=True)
    gathered = gathered.reshape(tp_size, dp_size, capacity, slice_width)
    expert_out = jnp.sum(gathered.astype(jnp.float32), axis=0).astype(jnp.bfloat16)
    returned = lax.all_to_all(expert_out, "dp", split_axis=0, concat_axis=0, tiled=True)
    shares = route_weights.astype(jnp.float32)
    shares = shares / jnp.sum(shares, axis=1, keepdims=True)
    slot_grid = slot_ids.reshape(token_count, top_count)
    slot_weight = jnp.sum(
        jnp.where(slot_grid[:, :, None] == slot_pos[None, None, :], shares[:, :, None], 0.0), axis=1
    )
    slot_weight = jnp.broadcast_to(slot_weight[None], (tp_size,) + slot_weight.shape)
    spread = jnp.einsum(
        "cts,sd->ctd",
        slot_weight,
        returned.reshape(experts * capacity, slice_width).astype(jnp.float32),
        precision=lax.Precision.HIGHEST,
        preferred_element_type=jnp.float32,
    ).astype(jnp.bfloat16)
    expert_mix = lax.all_to_all(spread, "tp", split_axis=0, concat_axis=0, tiled=True)
    expert_mix = jnp.transpose(expert_mix, (1, 0, 2)).reshape(token_count, model_width)
    attended = attend_local(
        queries, key_codes, key_scales, cache_values, new_keys, new_values, lengths
    )
    return (expert_mix, attended)


def solution(mesh):
    placed = (
        P("dp", None),
        P("dp", None),
        P("dp", None),
        P("dp", None, "tp"),
        P("dp", None, "tp"),
        P("dp", "tp", None),
        P("dp", "tp"),
        P("dp", "tp"),
        P("tp", "dp"),
        P("dp", "tp"),
        P("dp", "tp"),
        P("dp", "tp"),
        P("dp"),
    )
    return jax.shard_map(
        on_device,
        mesh=mesh,
        in_specs=placed,
        out_specs=(P("dp", None), P("dp", "tp")),
        check_vma=False,
    )
```

```python
import jax
import jax.numpy as jnp
from jax import lax
from jax.sharding import PartitionSpec as P
from jax.experimental import pallas as pl
from jax.experimental.pallas import tpu as pltpu

rope_base = 1000000.0


def inverse_freq(head_size):
    steps = jnp.arange(head_size // 2, dtype=jnp.float32) * (2.0 / head_size)
    return jnp.exp(-steps * jnp.log(jnp.float32(rope_base)))


def rotate(vector, angles):
    half_size = vector.shape[-1] // 2
    front_half = vector[..., :half_size]
    back_half = vector[..., half_size:]
    cosine = jnp.cos(angles)
    sine_part = jnp.sin(angles)
    return jnp.concatenate(
        [front_half * cosine - back_half * sine_part, back_half * cosine + front_half * sine_part],
        axis=-1,
    )


def attend_local(queries, codes, scales, cache_values, new_keys, new_values, lengths):
    row_count = queries.shape[0]
    cache_len = codes.shape[0]
    groups = scales.shape[0]
    head_size = codes.shape[1] // groups
    per_group = queries.shape[1] // (groups * head_size)
    request_end = jnp.cumsum(lengths)
    starts = request_end - lengths
    cache_pos = jnp.arange(cache_len, dtype=jnp.int32)
    member = (cache_pos[:, None] >= starts[None, :]) & (cache_pos[:, None] < request_end[None, :])
    offset = jnp.sum(jnp.where(member, starts[None, :], 0), axis=1)
    position = (cache_pos - offset).astype(jnp.float32)
    frequency = inverse_freq(head_size)
    cache_keys = (
        codes.astype(jnp.float32).reshape(cache_len, groups, head_size)
        * jnp.transpose(scales)[:, :, None]
    )
    cache_keys = rotate(cache_keys, position[:, None, None] * frequency[None, None, :]).astype(
        jnp.bfloat16
    )
    query_angles = lengths.astype(jnp.float32)[:, None] * frequency[None, :]
    rotated_query = queries.astype(jnp.float32).reshape(row_count, groups, per_group, head_size)
    rotated_query = rotate(rotated_query, query_angles[:, None, None, :]).astype(jnp.bfloat16)
    fresh_key = rotate(
        new_keys.astype(jnp.float32).reshape(row_count, groups, head_size), query_angles[:, None, :]
    ).astype(jnp.bfloat16)
    score_scale = head_size ** (-0.5)
    scores = (
        jnp.einsum("rgqd,cgd->rgqc", rotated_query, cache_keys, preferred_element_type=jnp.float32)
        * score_scale
    )
    own_score = (
        jnp.einsum("rgqd,rgd->rgq", rotated_query, fresh_key, preferred_element_type=jnp.float32)
        * score_scale
    )
    live_mask = jnp.transpose(member)[:, None, None, :]
    scores = jnp.where(live_mask, scores, -jnp.inf)
    peak_score = jnp.maximum(jnp.max(scores, axis=-1), own_score)
    weights = jnp.exp(scores - peak_score[..., None])
    own_weight = jnp.exp(own_score - peak_score)
    weight_sum = jnp.sum(weights, axis=-1) + own_weight
    value_rows = cache_values.reshape(cache_len, groups, head_size)
    mixture = jnp.einsum(
        "rgqc,cgd->rgqd",
        weights.astype(jnp.bfloat16),
        value_rows,
        preferred_element_type=jnp.float32,
    )
    mixture = mixture + own_weight[..., None] * new_values.astype(jnp.float32).reshape(
        row_count, groups, 1, head_size
    )
    return (
        (mixture / weight_sum[..., None])
        .reshape(row_count, groups * per_group * head_size)
        .astype(jnp.bfloat16)
    )


def expert_kernel(x_ref, gate_ref, up_ref, down_ref, out_ref, acc_ref):
    step = pl.program_id(0)
    inputs = x_ref[...]
    gate_act = jnp.dot(inputs, gate_ref[...], preferred_element_type=jnp.float32)
    up_act = jnp.dot(inputs, up_ref[...], preferred_element_type=jnp.float32)
    hidden_act = (gate_act / (1.0 + jnp.exp(-gate_act)) * up_act).astype(jnp.bfloat16)
    partial_value = jnp.dot(hidden_act, down_ref[...], preferred_element_type=jnp.float32)

    @pl.when(step == 0)
    def _():
        acc_ref[...] = partial_value

    @pl.when(step > 0)
    def _():
        acc_ref[...] += partial_value

    @pl.when(step == pl.num_programs(0) - 1)
    def _():
        pieces = out_ref.shape[0]
        width = out_ref.shape[2]
        for piece in range(pieces):
            out_ref[piece] = acc_ref[:, piece * width:(piece + 1) * width].astype(out_ref.dtype)


def expert_ffn(inputs, gate_w, up_w, down_w, pieces):
    rows, model_width = inputs.shape
    hidden_width = gate_w.shape[1]
    chunk = 128 if hidden_width % 128 == 0 else hidden_width
    width = down_w.shape[1] // pieces
    return pl.pallas_call(
        expert_kernel,
        out_shape=jax.ShapeDtypeStruct((pieces, rows, width), jnp.bfloat16),
        grid=(hidden_width // chunk,),
        in_specs=[
            pl.BlockSpec((rows, model_width), lambda i: (0, 0)),
            pl.BlockSpec((model_width, chunk), lambda i: (0, i)),
            pl.BlockSpec((model_width, chunk), lambda i: (0, i)),
            pl.BlockSpec((chunk, down_w.shape[1]), lambda i: (i, 0)),
        ],
        out_specs=pl.BlockSpec((pieces, rows, width), lambda i: (0, 0, 0)),
        scratch_shapes=[pltpu.VMEM((rows, down_w.shape[1]), jnp.float32)],
        compiler_params=pltpu.CompilerParams(dimension_semantics=("arbitrary",)),
    )(inputs, gate_w, up_w, down_w)


def expert_block(arrived, w_gate, w_up, w_down):
    arrived_shape = arrived.shape
    inputs = arrived.reshape(-1, arrived_shape[-1])
    gate_act = jnp.dot(inputs, w_gate[0], preferred_element_type=jnp.float32)
    up_act = jnp.dot(inputs, w_up[0], preferred_element_type=jnp.float32)
    hidden_act = (jax.nn.silu(gate_act) * up_act).astype(jnp.bfloat16)
    partial_value = jnp.dot(hidden_act, w_down[0], preferred_element_type=jnp.float32)
    return partial_value.reshape(arrived_shape[0], arrived_shape[1], partial_value.shape[-1])


def on_device(
    hidden,
    routes,
    route_weights,
    w_gate,
    w_up,
    w_down,
    queries,
    key_codes,
    key_scales,
    cache_values,
    new_keys,
    new_values,
    lengths,
):
    token_count = routes.shape[0]
    top_count = routes.shape[1]
    model_width = hidden.shape[1]
    tp_size = lax.axis_size("tp")
    dp_size = lax.axis_size("dp")
    slice_width = model_width // tp_size
    experts = dp_size * w_gate.shape[0]
    capacity = min(token_count, max(2, token_count * top_count * 2 // experts))
    flat_ids = routes.reshape(-1)
    pair_count = flat_ids.shape[0]
    pair_pos = jnp.arange(pair_count, dtype=jnp.int32)
    same_before = (flat_ids[:, None] == flat_ids[None, :]) & (pair_pos[None, :] < pair_pos[:, None])
    rank_ids = jnp.sum(same_before.astype(jnp.int32), axis=1)
    slot_ids = flat_ids * capacity + rank_ids
    slot_pos = jnp.arange(experts * capacity, dtype=jnp.int32)
    token_of_pair = pair_pos // top_count
    token_pos = jnp.arange(token_count, dtype=jnp.int32)
    slot_hit = slot_pos[:, None] == slot_ids[None, :]
    slot_token = jnp.sum(jnp.where(slot_hit, token_of_pair[None, :], 0), axis=1)
    slot_token = jnp.where(jnp.any(slot_hit, axis=1), slot_token, token_count)
    selector = (slot_token[:, None] == token_pos[None, :]).astype(hidden.dtype)
    outgoing = jnp.dot(selector, hidden, preferred_element_type=jnp.float32).astype(hidden.dtype)
    outgoing = outgoing.reshape(experts, capacity, model_width)
    arrived = lax.all_to_all(outgoing, "dp", split_axis=0, concat_axis=0, tiled=True)
    slots = dp_size * capacity
    partial_value = expert_ffn(
        arrived.reshape(slots, model_width), w_gate[0], w_up[0], w_down[0], tp_size
    )
    gathered = lax.all_to_all(partial_value, "tp", split_axis=0, concat_axis=0, tiled=True)
    gathered = gathered.reshape(tp_size, dp_size, capacity, slice_width)
    expert_out = jnp.sum(gathered.astype(jnp.float32), axis=0).astype(jnp.bfloat16)
    returned = lax.all_to_all(expert_out, "dp", split_axis=0, concat_axis=0, tiled=True)
    shares = route_weights.astype(jnp.float32)
    shares = shares / jnp.sum(shares, axis=1, keepdims=True)
    slot_grid = slot_ids.reshape(token_count, top_count)
    slot_weight = jnp.sum(
        jnp.where(slot_grid[:, :, None] == slot_pos[None, None, :], shares[:, :, None], 0.0), axis=1
    )
    slot_weight = jnp.broadcast_to(slot_weight[None], (tp_size,) + slot_weight.shape)
    spread = jnp.einsum(
        "cts,sd->ctd",
        slot_weight,
        returned.reshape(experts * capacity, slice_width).astype(jnp.float32),
        precision=lax.Precision.HIGHEST,
        preferred_element_type=jnp.float32,
    ).astype(jnp.bfloat16)
    expert_mix = lax.all_to_all(spread, "tp", split_axis=0, concat_axis=0, tiled=True)
    expert_mix = jnp.transpose(expert_mix, (1, 0, 2)).reshape(token_count, model_width)
    attended = attend_local(
        queries, key_codes, key_scales, cache_values, new_keys, new_values, lengths
    )
    return (expert_mix, attended)


def solution(mesh):
    placed = (
        P("dp", None),
        P("dp", None),
        P("dp", None),
        P("dp", None, "tp"),
        P("dp", None, "tp"),
        P("dp", "tp", None),
        P("dp", "tp"),
        P("dp", "tp"),
        P("tp", "dp"),
        P("dp", "tp"),
        P("dp", "tp"),
        P("dp", "tp"),
        P("dp"),
    )
    return jax.shard_map(
        on_device,
        mesh=mesh,
        in_specs=placed,
        out_specs=(P("dp", None), P("dp", "tp")),
        check_vma=False,
    )
```

```python
import jax
import jax.numpy as jnp
from jax import lax
from jax.sharding import PartitionSpec as P

rope_base = 1000000.0


def inverse_freq(head_size):
    steps = jnp.arange(head_size // 2, dtype=jnp.float32) * (2.0 / head_size)
    return jnp.exp(-steps * jnp.log(jnp.float32(rope_base)))


def rotate(vector, angles):
    half_size = vector.shape[-1] // 2
    front_half = vector[..., :half_size]
    back_half = vector[..., half_size:]
    cosine = jnp.cos(angles)
    sine_part = jnp.sin(angles)
    return jnp.concatenate(
        [front_half * cosine - back_half * sine_part, back_half * cosine + front_half * sine_part],
        axis=-1,
    )


def attend_local(queries, codes, scales, cache_values, new_keys, new_values, lengths):
    row_count = queries.shape[0]
    cache_len = codes.shape[0]
    groups = scales.shape[0]
    head_size = codes.shape[1] // groups
    per_group = queries.shape[1] // (groups * head_size)
    request_end = jnp.cumsum(lengths)
    starts = request_end - lengths
    cache_pos = jnp.arange(cache_len, dtype=jnp.int32)
    member = (cache_pos[:, None] >= starts[None, :]) & (cache_pos[:, None] < request_end[None, :])
    offset = jnp.sum(jnp.where(member, starts[None, :], 0), axis=1)
    position = (cache_pos - offset).astype(jnp.float32)
    frequency = inverse_freq(head_size)
    cache_keys = (
        codes.astype(jnp.float32).reshape(cache_len, groups, head_size)
        * jnp.transpose(scales)[:, :, None]
    )
    cache_keys = rotate(cache_keys, position[:, None, None] * frequency[None, None, :]).astype(
        jnp.bfloat16
    )
    query_angles = lengths.astype(jnp.float32)[:, None] * frequency[None, :]
    rotated_query = queries.astype(jnp.float32).reshape(row_count, groups, per_group, head_size)
    rotated_query = rotate(rotated_query, query_angles[:, None, None, :]).astype(jnp.bfloat16)
    fresh_key = rotate(
        new_keys.astype(jnp.float32).reshape(row_count, groups, head_size), query_angles[:, None, :]
    ).astype(jnp.bfloat16)
    score_scale = head_size ** (-0.5)
    scores = (
        jnp.einsum("rgqd,cgd->rgqc", rotated_query, cache_keys, preferred_element_type=jnp.float32)
        * score_scale
    )
    own_score = (
        jnp.einsum("rgqd,rgd->rgq", rotated_query, fresh_key, preferred_element_type=jnp.float32)
        * score_scale
    )
    live_mask = jnp.transpose(member)[:, None, None, :]
    scores = jnp.where(live_mask, scores, -jnp.inf)
    peak_score = jnp.maximum(jnp.max(scores, axis=-1), own_score)
    weights = jnp.exp(scores - peak_score[..., None])
    own_weight = jnp.exp(own_score - peak_score)
    weight_sum = jnp.sum(weights, axis=-1) + own_weight
    value_rows = cache_values.reshape(cache_len, groups, head_size)
    mixture = jnp.einsum(
        "rgqc,cgd->rgqd",
        weights.astype(jnp.bfloat16),
        value_rows,
        preferred_element_type=jnp.float32,
    )
    mixture = mixture + own_weight[..., None] * new_values.astype(jnp.float32).reshape(
        row_count, groups, 1, head_size
    )
    return (
        (mixture / weight_sum[..., None])
        .reshape(row_count, groups * per_group * head_size)
        .astype(jnp.bfloat16)
    )


def expert_block(arrived, w_gate, w_up, w_down):
    arrived_shape = arrived.shape
    inputs = arrived.reshape(-1, arrived_shape[-1])
    gate_act = jnp.dot(inputs, w_gate[0], preferred_element_type=jnp.float32)
    up_act = jnp.dot(inputs, w_up[0], preferred_element_type=jnp.float32)
    hidden_act = (jax.nn.silu(gate_act) * up_act).astype(jnp.bfloat16)
    partial_value = jnp.dot(hidden_act, w_down[0], preferred_element_type=jnp.float32)
    return partial_value.reshape(arrived_shape[0], arrived_shape[1], partial_value.shape[-1])


def on_device(
    hidden,
    routes,
    route_weights,
    w_gate,
    w_up,
    w_down,
    queries,
    key_codes,
    key_scales,
    cache_values,
    new_keys,
    new_values,
    lengths,
):
    token_count = routes.shape[0]
    top_count = routes.shape[1]
    model_width = hidden.shape[1]
    tp_size = lax.axis_size("tp")
    dp_size = lax.axis_size("dp")
    slice_width = model_width // tp_size
    experts = dp_size * w_gate.shape[0]
    capacity = min(token_count, max(2, token_count * top_count * 2 // experts))
    flat_ids = routes.reshape(-1)
    pair_count = flat_ids.shape[0]
    pair_pos = jnp.arange(pair_count, dtype=jnp.int32)
    same_before = (flat_ids[:, None] == flat_ids[None, :]) & (pair_pos[None, :] < pair_pos[:, None])
    rank_ids = jnp.sum(same_before.astype(jnp.int32), axis=1)
    slot_ids = flat_ids * capacity + rank_ids
    slot_pos = jnp.arange(experts * capacity, dtype=jnp.int32)
    token_of_pair = pair_pos // top_count
    token_pos = jnp.arange(token_count, dtype=jnp.int32)
    slot_hit = slot_pos[:, None] == slot_ids[None, :]
    slot_token = jnp.sum(jnp.where(slot_hit, token_of_pair[None, :], 0), axis=1)
    slot_token = jnp.where(jnp.any(slot_hit, axis=1), slot_token, token_count)
    selector = (slot_token[:, None] == token_pos[None, :]).astype(hidden.dtype)
    outgoing = jnp.dot(selector, hidden, preferred_element_type=jnp.float32).astype(hidden.dtype)
    outgoing = outgoing.reshape(experts, capacity, model_width)
    arrived = lax.all_to_all(outgoing, "dp", split_axis=0, concat_axis=0, tiled=True)
    slots = dp_size * capacity
    hidden_width = w_gate.shape[2]
    gate_up_w = jnp.concatenate([w_gate[0], w_up[0]], axis=1)
    gate_up = jnp.einsum("ecd,dh->ech", arrived, gate_up_w, preferred_element_type=jnp.float32)
    gate_act = gate_up[..., :hidden_width]
    up_act = gate_up[..., hidden_width:]
    hidden_act = (jax.nn.silu(gate_act) * up_act).astype(jnp.bfloat16).reshape(slots, -1)
    down_w = w_down[0].reshape(w_down.shape[1], tp_size, slice_width)
    partial_value = jnp.einsum("sh,hcd->csd", hidden_act, down_w, preferred_element_type=jnp.float32)
    partial_value = partial_value.astype(jnp.bfloat16)
    gathered = lax.all_to_all(partial_value, "tp", split_axis=0, concat_axis=0, tiled=True)
    expert_out = jnp.sum(gathered.astype(jnp.float32), axis=0).astype(jnp.bfloat16)
    expert_out = expert_out.reshape(dp_size, capacity, slice_width)
    returned = lax.all_to_all(expert_out, "dp", split_axis=0, concat_axis=0, tiled=True)
    shares = route_weights.astype(jnp.float32)
    shares = shares / jnp.sum(shares, axis=1, keepdims=True)
    slot_grid = slot_ids.reshape(token_count, top_count)
    slot_weight = jnp.sum(
        jnp.where(slot_grid[:, :, None] == slot_pos[None, None, :], shares[:, :, None], 0.0), axis=1
    )
    mix_cols = jnp.dot(
        slot_weight,
        returned.reshape(experts * capacity, slice_width).astype(jnp.float32),
        precision=lax.Precision.HIGHEST,
        preferred_element_type=jnp.float32,
    ).astype(jnp.bfloat16)
    spread = jnp.broadcast_to(mix_cols[:, None, :], (token_count, tp_size, slice_width))
    expert_mix = lax.all_to_all(spread, "tp", split_axis=1, concat_axis=1, tiled=True)
    expert_mix = expert_mix.reshape(token_count, model_width)
    attended = attend_local(
        queries, key_codes, key_scales, cache_values, new_keys, new_values, lengths
    )
    return (expert_mix, attended)


def solution(mesh):
    placed = (
        P("dp", None),
        P("dp", None),
        P("dp", None),
        P("dp", None, "tp"),
        P("dp", None, "tp"),
        P("dp", "tp", None),
        P("dp", "tp"),
        P("dp", "tp"),
        P("tp", "dp"),
        P("dp", "tp"),
        P("dp", "tp"),
        P("dp", "tp"),
        P("dp"),
    )
    return jax.shard_map(
        on_device,
        mesh=mesh,
        in_specs=placed,
        out_specs=(P("dp", None), P("dp", "tp")),
        check_vma=False,
    )
```

```python
import jax
import jax.numpy as jnp
from jax import lax
from jax.sharding import PartitionSpec as P

rope_base = 1000000.0


def inverse_freq(head_size):
    steps = jnp.arange(head_size // 2, dtype=jnp.float32) * (2.0 / head_size)
    return jnp.exp(-steps * jnp.log(jnp.float32(rope_base)))


def rotate(vector, angles):
    half_size = vector.shape[-1] // 2
    front_half = vector[..., :half_size]
    back_half = vector[..., half_size:]
    cosine = jnp.cos(angles)
    sine_part = jnp.sin(angles)
    return jnp.concatenate(
        [front_half * cosine - back_half * sine_part, back_half * cosine + front_half * sine_part],
        axis=-1,
    )


def attend_local(queries, codes, scales, cache_values, new_keys, new_values, lengths):
    row_count = queries.shape[0]
    cache_len = codes.shape[0]
    groups = scales.shape[0]
    head_size = codes.shape[1] // groups
    per_group = queries.shape[1] // (groups * head_size)
    request_end = jnp.cumsum(lengths)
    starts = request_end - lengths
    cache_pos = jnp.arange(cache_len, dtype=jnp.int32)
    member = (cache_pos[:, None] >= starts[None, :]) & (cache_pos[:, None] < request_end[None, :])
    offset = jnp.sum(jnp.where(member, starts[None, :], 0), axis=1)
    position = (cache_pos - offset).astype(jnp.float32)
    frequency = inverse_freq(head_size)
    cache_keys = (
        codes.astype(jnp.float32).reshape(cache_len, groups, head_size)
        * jnp.transpose(scales)[:, :, None]
    )
    cache_keys = rotate(cache_keys, position[:, None, None] * frequency[None, None, :]).astype(
        jnp.bfloat16
    )
    query_angles = lengths.astype(jnp.float32)[:, None] * frequency[None, :]
    rotated_query = queries.astype(jnp.float32).reshape(row_count, groups, per_group, head_size)
    rotated_query = rotate(rotated_query, query_angles[:, None, None, :]).astype(jnp.bfloat16)
    fresh_key = rotate(
        new_keys.astype(jnp.float32).reshape(row_count, groups, head_size), query_angles[:, None, :]
    ).astype(jnp.bfloat16)
    score_scale = head_size ** (-0.5)
    scores = (
        jnp.einsum("rgqd,cgd->rgqc", rotated_query, cache_keys, preferred_element_type=jnp.float32)
        * score_scale
    )
    own_score = (
        jnp.einsum("rgqd,rgd->rgq", rotated_query, fresh_key, preferred_element_type=jnp.float32)
        * score_scale
    )
    live_mask = jnp.transpose(member)[:, None, None, :]
    scores = jnp.where(live_mask, scores, -jnp.inf)
    peak_score = jnp.maximum(jnp.max(scores, axis=-1), own_score)
    weights = jnp.exp(scores - peak_score[..., None])
    own_weight = jnp.exp(own_score - peak_score)
    weight_sum = jnp.sum(weights, axis=-1) + own_weight
    value_rows = cache_values.reshape(cache_len, groups, head_size)
    mixture = jnp.einsum(
        "rgqc,cgd->rgqd",
        weights.astype(jnp.bfloat16),
        value_rows,
        preferred_element_type=jnp.float32,
    )
    mixture = mixture + own_weight[..., None] * new_values.astype(jnp.float32).reshape(
        row_count, groups, 1, head_size
    )
    return (
        (mixture / weight_sum[..., None])
        .reshape(row_count, groups * per_group * head_size)
        .astype(jnp.bfloat16)
    )


def expert_block(arrived, w_gate, w_up, w_down):
    arrived_shape = arrived.shape
    inputs = arrived.reshape(-1, arrived_shape[-1])
    gate_act = jnp.dot(inputs, w_gate[0], preferred_element_type=jnp.float32)
    up_act = jnp.dot(inputs, w_up[0], preferred_element_type=jnp.float32)
    hidden_act = (jax.nn.silu(gate_act) * up_act).astype(jnp.bfloat16)
    partial_value = jnp.dot(hidden_act, w_down[0], preferred_element_type=jnp.float32)
    return partial_value.reshape(arrived_shape[0], arrived_shape[1], partial_value.shape[-1])


def on_device(
    hidden,
    routes,
    route_weights,
    w_gate,
    w_up,
    w_down,
    queries,
    key_codes,
    key_scales,
    cache_values,
    new_keys,
    new_values,
    lengths,
):
    token_count = routes.shape[0]
    top_count = routes.shape[1]
    model_width = hidden.shape[1]
    tp_size = lax.axis_size("tp")
    dp_size = lax.axis_size("dp")
    slice_width = model_width // tp_size
    experts = dp_size * w_gate.shape[0]
    capacity = min(token_count, max(2, token_count * top_count * 2 // experts))
    expert_pos = jnp.arange(experts, dtype=jnp.int32)
    token_pos = jnp.arange(token_count, dtype=jnp.int32)
    chose = jnp.any(routes[:, :, None] == expert_pos[None, None, :], axis=1)
    first_token = jnp.min(jnp.where(chose, token_pos[:, None], token_count), axis=0)
    last_token = jnp.max(jnp.where(chose, token_pos[:, None], -1), axis=0)
    second_token = jnp.where(last_token > first_token, last_token, token_count)
    slot_token = jnp.stack([first_token, second_token], axis=1).reshape(-1)
    rank_grid = (token_pos[:, None] != first_token[routes]).astype(jnp.int32)
    slot_ids = (routes * capacity + rank_grid).reshape(-1)
    slot_pos = jnp.arange(experts * capacity, dtype=jnp.int32)
    selector = (slot_token[:, None] == token_pos[None, :]).astype(hidden.dtype)
    outgoing = jnp.dot(selector, hidden, preferred_element_type=jnp.float32).astype(hidden.dtype)
    outgoing = outgoing.reshape(experts, capacity, model_width)
    arrived = lax.all_to_all(outgoing, "dp", split_axis=0, concat_axis=0, tiled=True)
    slots = dp_size * capacity
    hidden_width = w_gate.shape[2]
    gate_up_w = jnp.concatenate([w_gate[0], w_up[0]], axis=1)
    gate_up = jnp.einsum("ecd,dh->ech", arrived, gate_up_w, preferred_element_type=jnp.float32)
    gate_act = gate_up[..., :hidden_width]
    up_act = gate_up[..., hidden_width:]
    hidden_act = (jax.nn.silu(gate_act) * up_act).astype(jnp.bfloat16).reshape(slots, -1)
    down_w = w_down[0].reshape(w_down.shape[1], tp_size, slice_width)
    partial_value = jnp.einsum("sh,hcd->csd", hidden_act, down_w, preferred_element_type=jnp.float32)
    partial_value = partial_value.astype(jnp.bfloat16)
    gathered = lax.all_to_all(partial_value, "tp", split_axis=0, concat_axis=0, tiled=True)
    expert_out = jnp.sum(gathered.astype(jnp.float32), axis=0).astype(jnp.bfloat16)
    expert_out = expert_out.reshape(dp_size, capacity, slice_width)
    returned = lax.all_to_all(expert_out, "dp", split_axis=0, concat_axis=0, tiled=True)
    shares = route_weights.astype(jnp.float32)
    shares = shares / jnp.sum(shares, axis=1, keepdims=True)
    slot_grid = slot_ids.reshape(token_count, top_count)
    slot_weight = jnp.sum(
        jnp.where(slot_grid[:, :, None] == slot_pos[None, None, :], shares[:, :, None], 0.0), axis=1
    )
    mix_cols = jnp.dot(
        slot_weight,
        returned.reshape(experts * capacity, slice_width).astype(jnp.float32),
        precision=lax.Precision.HIGHEST,
        preferred_element_type=jnp.float32,
    ).astype(jnp.bfloat16)
    spread = jnp.broadcast_to(mix_cols[:, None, :], (token_count, tp_size, slice_width))
    expert_mix = lax.all_to_all(spread, "tp", split_axis=1, concat_axis=1, tiled=True)
    expert_mix = expert_mix.reshape(token_count, model_width)
    attended = attend_local(
        queries, key_codes, key_scales, cache_values, new_keys, new_values, lengths
    )
    return (expert_mix, attended)


def solution(mesh):
    placed = (
        P("dp", None),
        P("dp", None),
        P("dp", None),
        P("dp", None, "tp"),
        P("dp", None, "tp"),
        P("dp", "tp", None),
        P("dp", "tp"),
        P("dp", "tp"),
        P("tp", "dp"),
        P("dp", "tp"),
        P("dp", "tp"),
        P("dp", "tp"),
        P("dp"),
    )
    return jax.shard_map(
        on_device,
        mesh=mesh,
        in_specs=placed,
        out_specs=(P("dp", None), P("dp", "tp")),
        check_vma=False,
    )
```

```python
import jax
import jax.numpy as jnp
from jax import lax
from jax.sharding import PartitionSpec as P

rope_base = 1000000.0


def inverse_freq(head_size):
    steps = jnp.arange(head_size // 2, dtype=jnp.float32) * (2.0 / head_size)
    return jnp.exp(-steps * jnp.log(jnp.float32(rope_base)))


def rotate(vector, angles):
    half_size = vector.shape[-1] // 2
    front_half = vector[..., :half_size]
    back_half = vector[..., half_size:]
    cosine = jnp.cos(angles)
    sine_part = jnp.sin(angles)
    return jnp.concatenate(
        [front_half * cosine - back_half * sine_part, back_half * cosine + front_half * sine_part],
        axis=-1,
    )


def attend_local(queries, codes, scales, cache_values, new_keys, new_values, lengths):
    row_count = queries.shape[0]
    cache_len = codes.shape[0]
    groups = scales.shape[0]
    head_size = codes.shape[1] // groups
    per_group = queries.shape[1] // (groups * head_size)
    request_end = jnp.cumsum(lengths)
    starts = request_end - lengths
    cache_pos = jnp.arange(cache_len, dtype=jnp.int32)
    member = (cache_pos[:, None] >= starts[None, :]) & (cache_pos[:, None] < request_end[None, :])
    offset = jnp.sum(jnp.where(member, starts[None, :], 0), axis=1)
    position = (cache_pos - offset).astype(jnp.float32)
    frequency = inverse_freq(head_size)
    cache_keys = (
        codes.astype(jnp.float32).reshape(cache_len, groups, head_size)
        * jnp.transpose(scales)[:, :, None]
    )
    cache_keys = rotate(cache_keys, position[:, None, None] * frequency[None, None, :]).astype(
        jnp.bfloat16
    )
    query_angles = lengths.astype(jnp.float32)[:, None] * frequency[None, :]
    rotated_query = queries.astype(jnp.float32).reshape(row_count, groups, per_group, head_size)
    rotated_query = rotate(rotated_query, query_angles[:, None, None, :]).astype(jnp.bfloat16)
    fresh_key = rotate(
        new_keys.astype(jnp.float32).reshape(row_count, groups, head_size), query_angles[:, None, :]
    ).astype(jnp.bfloat16)
    score_scale = head_size ** (-0.5)
    scores = (
        jnp.einsum("rgqd,cgd->rgqc", rotated_query, cache_keys, preferred_element_type=jnp.float32)
        * score_scale
    )
    own_score = (
        jnp.einsum("rgqd,rgd->rgq", rotated_query, fresh_key, preferred_element_type=jnp.float32)
        * score_scale
    )
    live_mask = jnp.transpose(member)[:, None, None, :]
    scores = jnp.where(live_mask, scores, -jnp.inf)
    peak_score = jnp.maximum(jnp.max(scores, axis=-1), own_score)
    weights = jnp.exp(scores - peak_score[..., None])
    own_weight = jnp.exp(own_score - peak_score)
    weight_sum = jnp.sum(weights, axis=-1) + own_weight
    value_rows = cache_values.reshape(cache_len, groups, head_size)
    mixture = jnp.einsum(
        "rgqc,cgd->rgqd",
        weights.astype(jnp.bfloat16),
        value_rows,
        preferred_element_type=jnp.float32,
    )
    mixture = mixture + own_weight[..., None] * new_values.astype(jnp.float32).reshape(
        row_count, groups, 1, head_size
    )
    return (
        (mixture / weight_sum[..., None])
        .reshape(row_count, groups * per_group * head_size)
        .astype(jnp.bfloat16)
    )


def expert_block(arrived, w_gate, w_up, w_down):
    arrived_shape = arrived.shape
    inputs = arrived.reshape(-1, arrived_shape[-1])
    gate_act = jnp.dot(inputs, w_gate[0], preferred_element_type=jnp.float32)
    up_act = jnp.dot(inputs, w_up[0], preferred_element_type=jnp.float32)
    hidden_act = (jax.nn.silu(gate_act) * up_act).astype(jnp.bfloat16)
    partial_value = jnp.dot(hidden_act, w_down[0], preferred_element_type=jnp.float32)
    return partial_value.reshape(arrived_shape[0], arrived_shape[1], partial_value.shape[-1])


def on_device(
    hidden,
    routes,
    route_weights,
    w_gate,
    w_up,
    w_down,
    queries,
    key_codes,
    key_scales,
    cache_values,
    new_keys,
    new_values,
    lengths,
):
    token_count = routes.shape[0]
    top_count = routes.shape[1]
    model_width = hidden.shape[1]
    tp_size = lax.axis_size("tp")
    dp_size = lax.axis_size("dp")
    slice_width = model_width // tp_size
    experts = dp_size * w_gate.shape[0]
    capacity = min(token_count, max(2, token_count * top_count * 2 // experts))
    flat_ids = routes.reshape(-1)
    pair_count = flat_ids.shape[0]
    pair_pos = jnp.arange(pair_count, dtype=jnp.int32)
    same_before = (flat_ids[:, None] == flat_ids[None, :]) & (pair_pos[None, :] < pair_pos[:, None])
    rank_ids = jnp.sum(same_before.astype(jnp.int32), axis=1)
    slot_ids = flat_ids * capacity + rank_ids
    slot_pos = jnp.arange(experts * capacity, dtype=jnp.int32)
    token_of_pair = pair_pos // top_count
    token_pos = jnp.arange(token_count, dtype=jnp.int32)
    slot_hit = slot_pos[:, None] == slot_ids[None, :]
    slot_token = jnp.sum(jnp.where(slot_hit, token_of_pair[None, :], 0), axis=1)
    slot_token = jnp.where(jnp.any(slot_hit, axis=1), slot_token, token_count)
    selector = (slot_token[:, None] == token_pos[None, :]).astype(hidden.dtype)
    outgoing = jnp.dot(selector, hidden, preferred_element_type=jnp.float32).astype(hidden.dtype)
    outgoing = outgoing.reshape(experts, capacity, model_width)
    arrived = lax.all_to_all(outgoing, "dp", split_axis=0, concat_axis=0, tiled=True)
    slots = dp_size * capacity
    hidden_width = w_gate.shape[2]
    gate_up_w = jnp.concatenate([w_gate[0], w_up[0]], axis=1)
    gate_up = jnp.einsum("ecd,dh->ech", arrived, gate_up_w, preferred_element_type=jnp.float32)
    gate_act = gate_up[..., :hidden_width]
    up_act = gate_up[..., hidden_width:]
    hidden_act = (jax.nn.silu(gate_act) * up_act).astype(jnp.bfloat16).reshape(slots, -1)
    down_w = w_down[0].reshape(w_down.shape[1], tp_size, slice_width)
    partial_value = jnp.einsum("sh,hcd->csd", hidden_act, down_w, preferred_element_type=jnp.float32)
    partial_value = partial_value.astype(jnp.bfloat16)
    gathered = lax.all_to_all(partial_value, "tp", split_axis=0, concat_axis=0, tiled=True)
    expert_out = jnp.sum(gathered.astype(jnp.float32), axis=0).astype(jnp.bfloat16)
    expert_out = expert_out.reshape(dp_size, capacity, slice_width)
    returned = lax.all_to_all(expert_out, "dp", split_axis=0, concat_axis=0, tiled=True)
    shares = route_weights.astype(jnp.float32)
    shares = shares / jnp.sum(shares, axis=1, keepdims=True)
    slot_grid = slot_ids.reshape(token_count, top_count)
    slot_weight = jnp.sum(
        jnp.where(slot_grid[:, :, None] == slot_pos[None, None, :], shares[:, :, None], 0.0), axis=1
    )
    slot_weight = jnp.broadcast_to(slot_weight[None], (tp_size,) + slot_weight.shape)
    spread = jnp.einsum(
        "cts,sd->ctd",
        slot_weight,
        returned.reshape(experts * capacity, slice_width).astype(jnp.float32),
        precision=lax.Precision.HIGHEST,
        preferred_element_type=jnp.float32,
    ).astype(jnp.bfloat16)
    expert_mix = lax.all_to_all(spread, "tp", split_axis=0, concat_axis=0, tiled=True)
    expert_mix = jnp.transpose(expert_mix, (1, 0, 2)).reshape(token_count, model_width)
    attended = attend_local(
        queries, key_codes, key_scales, cache_values, new_keys, new_values, lengths
    )
    return (expert_mix, attended)


def solution(mesh):
    placed = (
        P("dp", None),
        P("dp", None),
        P("dp", None),
        P("dp", None, "tp"),
        P("dp", None, "tp"),
        P("dp", "tp", None),
        P("dp", "tp"),
        P("dp", "tp"),
        P("tp", "dp"),
        P("dp", "tp"),
        P("dp", "tp"),
        P("dp", "tp"),
        P("dp"),
    )
    return jax.shard_map(
        on_device,
        mesh=mesh,
        in_specs=placed,
        out_specs=(P("dp", None), P("dp", "tp")),
        check_vma=False,
    )
```

```python
import jax
import jax.numpy as jnp
from jax import lax
from jax.sharding import PartitionSpec as P

rope_base = 1000000.0


def inverse_freq(head_size):
    steps = jnp.arange(head_size // 2, dtype=jnp.float32) * (2.0 / head_size)
    return jnp.exp(-steps * jnp.log(jnp.float32(rope_base)))


def rotate(vector, angles):
    half_size = vector.shape[-1] // 2
    front_half = vector[..., :half_size]
    back_half = vector[..., half_size:]
    cosine = jnp.cos(angles)
    sine_part = jnp.sin(angles)
    return jnp.concatenate(
        [front_half * cosine - back_half * sine_part, back_half * cosine + front_half * sine_part],
        axis=-1,
    )


def attend_local(queries, codes, scales, cache_values, new_keys, new_values, lengths):
    row_count = queries.shape[0]
    cache_len = codes.shape[0]
    groups = scales.shape[0]
    head_size = codes.shape[1] // groups
    per_group = queries.shape[1] // (groups * head_size)
    request_end = jnp.cumsum(lengths)
    starts = request_end - lengths
    cache_pos = jnp.arange(cache_len, dtype=jnp.int32)
    member = (cache_pos[:, None] >= starts[None, :]) & (cache_pos[:, None] < request_end[None, :])
    offset = jnp.sum(jnp.where(member, starts[None, :], 0), axis=1)
    position = (cache_pos - offset).astype(jnp.float32)
    frequency = inverse_freq(head_size)
    cache_keys = (
        codes.astype(jnp.float32).reshape(cache_len, groups, head_size)
        * jnp.transpose(scales)[:, :, None]
    )
    cache_keys = rotate(cache_keys, position[:, None, None] * frequency[None, None, :]).astype(
        jnp.bfloat16
    )
    query_angles = lengths.astype(jnp.float32)[:, None] * frequency[None, :]
    rotated_query = queries.astype(jnp.float32).reshape(row_count, groups, per_group, head_size)
    rotated_query = rotate(rotated_query, query_angles[:, None, None, :]).astype(jnp.bfloat16)
    fresh_key = rotate(
        new_keys.astype(jnp.float32).reshape(row_count, groups, head_size), query_angles[:, None, :]
    ).astype(jnp.bfloat16)
    score_scale = head_size ** (-0.5)
    scores = (
        jnp.einsum("rgqd,cgd->rgqc", rotated_query, cache_keys, preferred_element_type=jnp.float32)
        * score_scale
    )
    own_score = (
        jnp.einsum("rgqd,rgd->rgq", rotated_query, fresh_key, preferred_element_type=jnp.float32)
        * score_scale
    )
    live_mask = jnp.transpose(member)[:, None, None, :]
    scores = jnp.where(live_mask, scores, -jnp.inf)
    peak_score = jnp.maximum(jnp.max(scores, axis=-1), own_score)
    weights = jnp.exp(scores - peak_score[..., None])
    own_weight = jnp.exp(own_score - peak_score)
    weight_sum = jnp.sum(weights, axis=-1) + own_weight
    value_rows = cache_values.reshape(cache_len, groups, head_size)
    mixture = jnp.einsum(
        "rgqc,cgd->rgqd",
        weights.astype(jnp.bfloat16),
        value_rows,
        preferred_element_type=jnp.float32,
    )
    mixture = mixture + own_weight[..., None] * new_values.astype(jnp.float32).reshape(
        row_count, groups, 1, head_size
    )
    return (
        (mixture / weight_sum[..., None])
        .reshape(row_count, groups * per_group * head_size)
        .astype(jnp.bfloat16)
    )


def expert_block(arrived, w_gate, w_up, w_down):
    arrived_shape = arrived.shape
    inputs = arrived.reshape(-1, arrived_shape[-1])
    gate_act = jnp.dot(inputs, w_gate[0], preferred_element_type=jnp.float32)
    up_act = jnp.dot(inputs, w_up[0], preferred_element_type=jnp.float32)
    hidden_act = (jax.nn.silu(gate_act) * up_act).astype(jnp.bfloat16)
    partial_value = jnp.dot(hidden_act, w_down[0], preferred_element_type=jnp.float32)
    return partial_value.reshape(arrived_shape[0], arrived_shape[1], partial_value.shape[-1])


def on_device(
    hidden,
    routes,
    route_weights,
    w_gate,
    w_up,
    w_down,
    queries,
    key_codes,
    key_scales,
    cache_values,
    new_keys,
    new_values,
    lengths,
):
    token_count = routes.shape[0]
    top_count = routes.shape[1]
    model_width = hidden.shape[1]
    tp_size = lax.axis_size("tp")
    dp_size = lax.axis_size("dp")
    slice_width = model_width // tp_size
    experts = dp_size * w_gate.shape[0]
    capacity = min(token_count, max(2, token_count * top_count * 2 // experts))
    flat_ids = routes.reshape(-1)
    pair_count = flat_ids.shape[0]
    pair_pos = jnp.arange(pair_count, dtype=jnp.int32)
    same_before = (flat_ids[:, None] == flat_ids[None, :]) & (pair_pos[None, :] < pair_pos[:, None])
    rank_ids = jnp.sum(same_before.astype(jnp.int32), axis=1)
    slot_ids = flat_ids * capacity + rank_ids
    slot_pos = jnp.arange(experts * capacity, dtype=jnp.int32)
    token_of_pair = pair_pos // top_count
    token_pos = jnp.arange(token_count, dtype=jnp.int32)
    slot_hit = slot_pos[:, None] == slot_ids[None, :]
    slot_token = jnp.sum(jnp.where(slot_hit, token_of_pair[None, :], 0), axis=1)
    slot_token = jnp.where(jnp.any(slot_hit, axis=1), slot_token, token_count)
    selector = (slot_token[:, None] == token_pos[None, :]).astype(hidden.dtype)
    outgoing = jnp.dot(selector, hidden, preferred_element_type=jnp.float32).astype(hidden.dtype)
    outgoing = outgoing.reshape(experts, capacity, model_width)
    arrived = lax.all_to_all(outgoing, "dp", split_axis=0, concat_axis=0, tiled=True)
    slots = dp_size * capacity
    hidden_width = w_gate.shape[2]
    gate_up_w = lax.optimization_barrier(jnp.concatenate([w_gate[0], w_up[0]], axis=1))
    gate_up = jnp.einsum("ecd,dh->ech", arrived, gate_up_w, preferred_element_type=jnp.float32)
    gate_act = gate_up[..., :hidden_width]
    up_act = gate_up[..., hidden_width:]
    hidden_act = (jax.nn.silu(gate_act) * up_act).astype(jnp.bfloat16).reshape(slots, -1)
    down_w = w_down[0].reshape(w_down.shape[1], tp_size, slice_width)
    partial_value = jnp.einsum("sh,hcd->csd", hidden_act, down_w, preferred_element_type=jnp.float32)
    partial_value = partial_value.astype(jnp.bfloat16)
    gathered = lax.all_to_all(partial_value, "tp", split_axis=0, concat_axis=0, tiled=True)
    expert_out = jnp.sum(gathered.astype(jnp.float32), axis=0).astype(jnp.bfloat16)
    expert_out = expert_out.reshape(dp_size, capacity, slice_width)
    returned = lax.all_to_all(expert_out, "dp", split_axis=0, concat_axis=0, tiled=True)
    shares = route_weights.astype(jnp.float32)
    shares = shares / jnp.sum(shares, axis=1, keepdims=True)
    slot_grid = slot_ids.reshape(token_count, top_count)
    slot_weight = jnp.sum(
        jnp.where(slot_grid[:, :, None] == slot_pos[None, None, :], shares[:, :, None], 0.0), axis=1
    )
    mix_cols = jnp.dot(
        slot_weight,
        returned.reshape(experts * capacity, slice_width).astype(jnp.float32),
        precision=lax.Precision.HIGHEST,
        preferred_element_type=jnp.float32,
    ).astype(jnp.bfloat16)
    spread = jnp.broadcast_to(mix_cols[:, None, :], (token_count, tp_size, slice_width))
    expert_mix = lax.all_to_all(spread, "tp", split_axis=1, concat_axis=1, tiled=True)
    expert_mix = expert_mix.reshape(token_count, model_width)
    attended = attend_local(
        queries, key_codes, key_scales, cache_values, new_keys, new_values, lengths
    )
    return (expert_mix, attended)


def solution(mesh):
    placed = (
        P("dp", None),
        P("dp", None),
        P("dp", None),
        P("dp", None, "tp"),
        P("dp", None, "tp"),
        P("dp", "tp", None),
        P("dp", "tp"),
        P("dp", "tp"),
        P("tp", "dp"),
        P("dp", "tp"),
        P("dp", "tp"),
        P("dp", "tp"),
        P("dp"),
    )
    return jax.shard_map(
        on_device,
        mesh=mesh,
        in_specs=placed,
        out_specs=(P("dp", None), P("dp", "tp")),
        check_vma=False,
    )
```

```python
import jax
import jax.numpy as jnp
from jax import lax
from jax.sharding import PartitionSpec as P

rope_base = 1000000.0


def inverse_freq(head_size):
    steps = jnp.arange(head_size // 2, dtype=jnp.float32) * (2.0 / head_size)
    return jnp.exp(-steps * jnp.log(jnp.float32(rope_base)))


def rotate(vector, angles):
    half_size = vector.shape[-1] // 2
    front_half = vector[..., :half_size]
    back_half = vector[..., half_size:]
    cosine = jnp.cos(angles)
    sine_part = jnp.sin(angles)
    return jnp.concatenate(
        [front_half * cosine - back_half * sine_part, back_half * cosine + front_half * sine_part],
        axis=-1,
    )


def attend_local(queries, codes, scales, cache_values, new_keys, new_values, lengths):
    row_count = queries.shape[0]
    cache_len = codes.shape[0]
    groups = scales.shape[0]
    head_size = codes.shape[1] // groups
    per_group = queries.shape[1] // (groups * head_size)
    request_end = jnp.cumsum(lengths)
    starts = request_end - lengths
    cache_pos = jnp.arange(cache_len, dtype=jnp.int32)
    member = (cache_pos[:, None] >= starts[None, :]) & (cache_pos[:, None] < request_end[None, :])
    offset = jnp.sum(jnp.where(member, starts[None, :], 0), axis=1)
    position = (cache_pos - offset).astype(jnp.float32)
    frequency = inverse_freq(head_size)
    cache_keys = (
        codes.astype(jnp.float32).reshape(cache_len, groups, head_size)
        * jnp.transpose(scales)[:, :, None]
    )
    cache_keys = rotate(cache_keys, position[:, None, None] * frequency[None, None, :]).astype(
        jnp.bfloat16
    )
    query_angles = lengths.astype(jnp.float32)[:, None] * frequency[None, :]
    rotated_query = queries.astype(jnp.float32).reshape(row_count, groups, per_group, head_size)
    rotated_query = rotate(rotated_query, query_angles[:, None, None, :]).astype(jnp.bfloat16)
    fresh_key = rotate(
        new_keys.astype(jnp.float32).reshape(row_count, groups, head_size), query_angles[:, None, :]
    ).astype(jnp.bfloat16)
    score_scale = head_size ** (-0.5)
    scores = (
        jnp.einsum("rgqd,cgd->rgqc", rotated_query, cache_keys, preferred_element_type=jnp.float32)
        * score_scale
    )
    own_score = (
        jnp.einsum("rgqd,rgd->rgq", rotated_query, fresh_key, preferred_element_type=jnp.float32)
        * score_scale
    )
    live_mask = jnp.transpose(member)[:, None, None, :]
    scores = jnp.where(live_mask, scores, -jnp.inf)
    peak_score = jnp.maximum(jnp.max(scores, axis=-1), own_score)
    weights = jnp.exp(scores - peak_score[..., None])
    own_weight = jnp.exp(own_score - peak_score)
    weight_sum = jnp.sum(weights, axis=-1) + own_weight
    value_rows = cache_values.reshape(cache_len, groups, head_size)
    mixture = jnp.einsum(
        "rgqc,cgd->rgqd",
        weights.astype(jnp.bfloat16),
        value_rows,
        preferred_element_type=jnp.float32,
    )
    mixture = mixture + own_weight[..., None] * new_values.astype(jnp.float32).reshape(
        row_count, groups, 1, head_size
    )
    return (
        (mixture / weight_sum[..., None])
        .reshape(row_count, groups * per_group * head_size)
        .astype(jnp.bfloat16)
    )


def expert_block(arrived, w_gate, w_up, w_down):
    arrived_shape = arrived.shape
    inputs = arrived.reshape(-1, arrived_shape[-1])
    gate_act = jnp.dot(inputs, w_gate[0], preferred_element_type=jnp.float32)
    up_act = jnp.dot(inputs, w_up[0], preferred_element_type=jnp.float32)
    hidden_act = (jax.nn.silu(gate_act) * up_act).astype(jnp.bfloat16)
    partial_value = jnp.dot(hidden_act, w_down[0], preferred_element_type=jnp.float32)
    return partial_value.reshape(arrived_shape[0], arrived_shape[1], partial_value.shape[-1])


def on_device(
    hidden,
    routes,
    route_weights,
    w_gate,
    w_up,
    w_down,
    queries,
    key_codes,
    key_scales,
    cache_values,
    new_keys,
    new_values,
    lengths,
):
    token_count = routes.shape[0]
    top_count = routes.shape[1]
    model_width = hidden.shape[1]
    tp_size = lax.axis_size("tp")
    dp_size = lax.axis_size("dp")
    slice_width = model_width // tp_size
    experts = dp_size * w_gate.shape[0]
    capacity = min(token_count, max(2, token_count * top_count * 2 // experts))
    flat_ids = routes.reshape(-1)
    pair_count = flat_ids.shape[0]
    pair_pos = jnp.arange(pair_count, dtype=jnp.int32)
    same_before = (flat_ids[:, None] == flat_ids[None, :]) & (pair_pos[None, :] < pair_pos[:, None])
    rank_ids = jnp.sum(same_before.astype(jnp.int32), axis=1)
    slot_ids = flat_ids * capacity + rank_ids
    slot_pos = jnp.arange(experts * capacity, dtype=jnp.int32)
    token_of_pair = pair_pos // top_count
    token_pos = jnp.arange(token_count, dtype=jnp.int32)
    slot_hit = slot_pos[:, None] == slot_ids[None, :]
    slot_token = jnp.sum(jnp.where(slot_hit, token_of_pair[None, :], 0), axis=1)
    slot_token = jnp.where(jnp.any(slot_hit, axis=1), slot_token, token_count)
    selector = (slot_token[:, None] == token_pos[None, :]).astype(hidden.dtype)
    outgoing = jnp.dot(selector, hidden, preferred_element_type=hidden.dtype)
    outgoing = outgoing.reshape(experts, capacity, model_width)
    arrived = lax.all_to_all(outgoing, "dp", split_axis=0, concat_axis=0, tiled=True)
    slots = dp_size * capacity
    hidden_width = w_gate.shape[2]
    gate_up_w = jnp.concatenate([w_gate[0], w_up[0]], axis=1)
    gate_up = jnp.einsum("ecd,dh->ech", arrived, gate_up_w, preferred_element_type=jnp.float32)
    gate_act = gate_up[..., :hidden_width]
    up_act = gate_up[..., hidden_width:]
    hidden_act = (jax.nn.silu(gate_act) * up_act).astype(jnp.bfloat16).reshape(slots, -1)
    down_w = w_down[0].reshape(w_down.shape[1], tp_size, slice_width)
    partial_value = jnp.einsum("sh,hcd->csd", hidden_act, down_w, preferred_element_type=jnp.float32)
    partial_value = partial_value.astype(jnp.bfloat16)
    gathered = lax.all_to_all(partial_value, "tp", split_axis=0, concat_axis=0, tiled=True)
    expert_out = jnp.sum(gathered.astype(jnp.float32), axis=0).astype(jnp.bfloat16)
    expert_out = expert_out.reshape(dp_size, capacity, slice_width)
    returned = lax.all_to_all(expert_out, "dp", split_axis=0, concat_axis=0, tiled=True)
    shares = route_weights.astype(jnp.float32)
    shares = shares / jnp.sum(shares, axis=1, keepdims=True)
    slot_grid = slot_ids.reshape(token_count, top_count)
    slot_weight = jnp.sum(
        jnp.where(slot_grid[:, :, None] == slot_pos[None, None, :], shares[:, :, None], 0.0), axis=1
    )
    mix_cols = jnp.dot(
        slot_weight,
        returned.reshape(experts * capacity, slice_width).astype(jnp.float32),
        precision=lax.Precision.HIGHEST,
        preferred_element_type=jnp.float32,
    ).astype(jnp.bfloat16)
    spread = jnp.broadcast_to(mix_cols[:, None, :], (token_count, tp_size, slice_width))
    expert_mix = lax.all_to_all(spread, "tp", split_axis=1, concat_axis=1, tiled=True)
    expert_mix = expert_mix.reshape(token_count, model_width)
    attended = attend_local(
        queries, key_codes, key_scales, cache_values, new_keys, new_values, lengths
    )
    return (expert_mix, attended)


def solution(mesh):
    placed = (
        P("dp", None),
        P("dp", None),
        P("dp", None),
        P("dp", None, "tp"),
        P("dp", None, "tp"),
        P("dp", "tp", None),
        P("dp", "tp"),
        P("dp", "tp"),
        P("tp", "dp"),
        P("dp", "tp"),
        P("dp", "tp"),
        P("dp", "tp"),
        P("dp"),
    )
    return jax.shard_map(
        on_device,
        mesh=mesh,
        in_specs=placed,
        out_specs=(P("dp", None), P("dp", "tp")),
        check_vma=False,
    )
```

```python
import jax
import jax.numpy as jnp
from jax import lax
from jax.sharding import PartitionSpec as P

rope_base = 1000000.0


def inverse_freq(head_size):
    steps = jnp.arange(head_size // 2, dtype=jnp.float32) * (2.0 / head_size)
    return jnp.exp(-steps * jnp.log(jnp.float32(rope_base)))


def rotate(vector, angles):
    half_size = vector.shape[-1] // 2
    front_half = vector[..., :half_size]
    back_half = vector[..., half_size:]
    cosine = jnp.cos(angles)
    sine_part = jnp.sin(angles)
    return jnp.concatenate(
        [front_half * cosine - back_half * sine_part, back_half * cosine + front_half * sine_part],
        axis=-1,
    )


def attend_local(queries, codes, scales, cache_values, new_keys, new_values, lengths):
    row_count = queries.shape[0]
    cache_len = codes.shape[0]
    groups = scales.shape[0]
    head_size = codes.shape[1] // groups
    per_group = queries.shape[1] // (groups * head_size)
    request_end = jnp.cumsum(lengths)
    starts = request_end - lengths
    cache_pos = jnp.arange(cache_len, dtype=jnp.int32)
    member = (cache_pos[:, None] >= starts[None, :]) & (cache_pos[:, None] < request_end[None, :])
    offset = jnp.sum(jnp.where(member, starts[None, :], 0), axis=1)
    position = (cache_pos - offset).astype(jnp.float32)
    frequency = inverse_freq(head_size)
    cache_keys = (
        codes.astype(jnp.float32).reshape(cache_len, groups, head_size)
        * jnp.transpose(scales)[:, :, None]
    )
    cache_keys = rotate(cache_keys, position[:, None, None] * frequency[None, None, :]).astype(
        jnp.bfloat16
    )
    query_angles = lengths.astype(jnp.float32)[:, None] * frequency[None, :]
    rotated_query = queries.astype(jnp.float32).reshape(row_count, groups, per_group, head_size)
    rotated_query = rotate(rotated_query, query_angles[:, None, None, :]).astype(jnp.bfloat16)
    fresh_key = rotate(
        new_keys.astype(jnp.float32).reshape(row_count, groups, head_size), query_angles[:, None, :]
    ).astype(jnp.bfloat16)
    score_scale = head_size ** (-0.5)
    scores = (
        jnp.einsum("rgqd,cgd->rgqc", rotated_query, cache_keys, preferred_element_type=jnp.float32)
        * score_scale
    )
    own_score = (
        jnp.einsum("rgqd,rgd->rgq", rotated_query, fresh_key, preferred_element_type=jnp.float32)
        * score_scale
    )
    live_mask = jnp.transpose(member)[:, None, None, :]
    scores = jnp.where(live_mask, scores, -jnp.inf)
    peak_score = jnp.maximum(jnp.max(scores, axis=-1), own_score)
    weights = jnp.exp(scores - peak_score[..., None])
    own_weight = jnp.exp(own_score - peak_score)
    weight_sum = jnp.sum(weights, axis=-1) + own_weight
    value_rows = cache_values.reshape(cache_len, groups, head_size)
    mixture = jnp.einsum(
        "rgqc,cgd->rgqd",
        weights.astype(jnp.bfloat16),
        value_rows,
        preferred_element_type=jnp.float32,
    )
    mixture = mixture + own_weight[..., None] * new_values.astype(jnp.float32).reshape(
        row_count, groups, 1, head_size
    )
    return (
        (mixture / weight_sum[..., None])
        .reshape(row_count, groups * per_group * head_size)
        .astype(jnp.bfloat16)
    )


def expert_block(arrived, w_gate, w_up, w_down):
    arrived_shape = arrived.shape
    inputs = arrived.reshape(-1, arrived_shape[-1])
    gate_act = jnp.dot(inputs, w_gate[0], preferred_element_type=jnp.float32)
    up_act = jnp.dot(inputs, w_up[0], preferred_element_type=jnp.float32)
    hidden_act = (jax.nn.silu(gate_act) * up_act).astype(jnp.bfloat16)
    partial_value = jnp.dot(hidden_act, w_down[0], preferred_element_type=jnp.float32)
    return partial_value.reshape(arrived_shape[0], arrived_shape[1], partial_value.shape[-1])


def on_device(
    hidden,
    routes,
    route_weights,
    w_gate,
    w_up,
    w_down,
    queries,
    key_codes,
    key_scales,
    cache_values,
    new_keys,
    new_values,
    lengths,
):
    token_count = routes.shape[0]
    top_count = routes.shape[1]
    model_width = hidden.shape[1]
    tp_size = lax.axis_size("tp")
    dp_size = lax.axis_size("dp")
    slice_width = model_width // tp_size
    experts = dp_size * w_gate.shape[0]
    capacity = min(token_count, max(2, token_count * top_count * 2 // experts))
    expert_pos = jnp.arange(experts, dtype=jnp.int32)
    token_pos = jnp.arange(token_count, dtype=jnp.int32)
    chose = jnp.any(routes[:, :, None] == expert_pos[None, None, :], axis=1)
    first_token = jnp.min(jnp.where(chose, token_pos[:, None], token_count), axis=0)
    last_token = jnp.max(jnp.where(chose, token_pos[:, None], -1), axis=0)
    second_token = jnp.where(last_token > first_token, last_token, token_count)
    slot_token = jnp.stack([first_token, second_token], axis=1).reshape(-1)
    rank_grid = (token_pos[:, None] != first_token[routes]).astype(jnp.int32)
    slot_ids = (routes * capacity + rank_grid).reshape(-1)
    slot_pos = jnp.arange(experts * capacity, dtype=jnp.int32)
    selector = (slot_token[:, None] == token_pos[None, :]).astype(hidden.dtype)
    outgoing = jnp.dot(selector, hidden, preferred_element_type=jnp.float32).astype(hidden.dtype)
    outgoing = outgoing.reshape(experts, capacity, model_width)
    arrived = lax.all_to_all(outgoing, "dp", split_axis=0, concat_axis=0, tiled=True)
    slots = dp_size * capacity
    hidden_width = w_gate.shape[2]
    gate_up_w = jnp.concatenate([w_gate[0], w_up[0]], axis=1)
    gate_up = jnp.einsum("ecd,dh->ech", arrived, gate_up_w, preferred_element_type=jnp.float32)
    gate_act = gate_up[..., :hidden_width]
    up_act = gate_up[..., hidden_width:]
    hidden_act = (jax.nn.silu(gate_act) * up_act).astype(jnp.bfloat16).reshape(slots, -1)
    down_w = w_down[0].reshape(w_down.shape[1], tp_size, slice_width)
    partial_value = jnp.einsum("sh,hcd->csd", hidden_act, down_w, preferred_element_type=jnp.float32)
    partial_value = partial_value.astype(jnp.bfloat16)
    gathered = lax.all_to_all(partial_value, "tp", split_axis=0, concat_axis=0, tiled=True)
    expert_out = jnp.sum(gathered.astype(jnp.float32), axis=0).astype(jnp.bfloat16)
    expert_out = expert_out.reshape(dp_size, capacity, slice_width)
    returned = lax.all_to_all(expert_out, "dp", split_axis=0, concat_axis=0, tiled=True)
    shares = route_weights.astype(jnp.float32)
    shares = shares / jnp.sum(shares, axis=1, keepdims=True)
    slot_grid = slot_ids.reshape(token_count, top_count)
    slot_weight = jnp.sum(
        jnp.where(slot_grid[:, :, None] == slot_pos[None, None, :], shares[:, :, None], 0.0), axis=1
    )
    slot_weight = jnp.broadcast_to(slot_weight[None], (tp_size,) + slot_weight.shape)
    spread = jnp.einsum(
        "cts,sd->ctd",
        slot_weight,
        returned.reshape(experts * capacity, slice_width).astype(jnp.float32),
        precision=lax.Precision.HIGHEST,
        preferred_element_type=jnp.float32,
    ).astype(jnp.bfloat16)
    expert_mix = lax.all_to_all(spread, "tp", split_axis=0, concat_axis=0, tiled=True)
    expert_mix = jnp.transpose(expert_mix, (1, 0, 2)).reshape(token_count, model_width)
    attended = attend_local(
        queries, key_codes, key_scales, cache_values, new_keys, new_values, lengths
    )
    return (expert_mix, attended)


def solution(mesh):
    placed = (
        P("dp", None),
        P("dp", None),
        P("dp", None),
        P("dp", None, "tp"),
        P("dp", None, "tp"),
        P("dp", "tp", None),
        P("dp", "tp"),
        P("dp", "tp"),
        P("tp", "dp"),
        P("dp", "tp"),
        P("dp", "tp"),
        P("dp", "tp"),
        P("dp"),
    )
    return jax.shard_map(
        on_device,
        mesh=mesh,
        in_specs=placed,
        out_specs=(P("dp", None), P("dp", "tp")),
        check_vma=False,
    )
```
